256 devices in a mesh: seq: 64 (over y, z, core), head: 4 (over x).
Axes of the slice: x: 4, y: 4, z: 8, core: 2. Of those that a mesh axis runs over, the one named last changes fastest.
Arguments:
- tokens: bfloat16 [2, 64, 4096], P(None, None, 'seq'), may hold values from -6 to 6
- lengths: int32 [64], replicated, may hold values from 1 to 32768, as said below
- page_owner: int32 [2048], P('seq'), may hold values from -1 to 63, as said below
- page_number: int32 [2048], P('seq'), may hold values from 0 to 511, as said below
- key_pages: bfloat16 [2048, 64, 4096], P('seq', None, 'head'), may hold values from -600 to 600
- value_pages: bfloat16 [2048, 64, 4096], P('seq', None, 'head'), may hold values from -6 to 6
- alibi_slopes: float32 [32], P('head'), as said below
- norm1_gain: float32 [4096], P('seq'), may hold values from 0.1 to 1.9
- norm2_gain: float32 [4096], P('seq'), may hold values from 0.1 to 1.9
- w_qkv: bfloat16 [4096, 3, 4096], P('seq', None, 'head'), may hold values from -0.09375 to 0.09375
- w_out: bfloat16 [4096, 4096], P('seq', 'head'), may hold values from -0.09375 to 0.09375
- w_up: bfloat16 [4096, 16384], P('seq', 'head'), may hold values from -0.09375 to 0.09375
- w_down: bfloat16 [4096, 16384], P('seq', 'head'), may hold values from -0.046875 to 0.046875
Outputs:
- layer_out: bfloat16 [2, 64, 4096], P(None, None, 'seq')
The draws below stay inside these ranges and needn't reach their ends.
Inputs may be any that keep to these rules, and one draw needn't show every extreme that they name: Exactly one request holds 32768 tokens; request r's cache fills page_number 0 .. ceil(lengths[r] / 64) - 1. `page_owner`: -1 marks a free slot; every page of every request stands in exactly one slot; on some indices of seq all 32 slots are used. `page_number`: 0 for free slots. `alibi_slopes`: Positive.
All inputs are finite; a program needn't handle non-finite values.
Results may differ from the reference program's by a relative error of at most 0.011.
Values may be sent and summed in bfloat16 or wider, within the bound.
No kernel may reach another device: no remote copies, remote signals or barrier semaphores. Data moves between devices by JAX's collectives and lax.ppermute only.
A program may use at most 128 MiB of HBM per device.

```python
import math
import jax
import jax.numpy as jnp
from jax import lax

D = 4096
NH = 32
HD = 128
FF = 16384
REQ = 64
STEPS = 2
PAGE = 64
PAGES_DEV = 32
BLK = 8
POOL = 2048
MAXLEN = 32768
SPREAD = 6


def page_table(base_key):
    split_keys = jax.random.split(jax.random.fold_in(base_key, 7), 6)
    longest_pages = MAXLEN // PAGE
    seq_count = POOL // PAGES_DEV
    half_count = seq_count // 2
    request_ids = jnp.arange(REQ, dtype=jnp.int32)
    extra_pages = jax.random.randint(split_keys[0], (REQ,), 0, 2 * SPREAD)
    long_request = jax.random.randint(split_keys[1], (), 0, REQ)
    page_counts = jnp.where(request_ids == long_request, longest_pages, 1 + extra_pages).astype(jnp.int32)
    tail_tokens = jax.random.randint(split_keys[2], (REQ,), 1, PAGE + 1)
    tail_tokens = jnp.where(request_ids == long_request, PAGE, tail_tokens)
    lengths = ((page_counts - 1) * PAGE + tail_tokens).astype(jnp.int32)
    page_ends = jnp.cumsum(page_counts).astype(jnp.int32)
    page_starts = page_ends - page_counts
    global_page = jnp.arange(POOL, dtype=jnp.int32)
    owner_list = jnp.sum((global_page[:, None] >= page_ends[None, :]).astype(jnp.int32), axis=1)
    live_page = global_page < page_ends[REQ - 1]
    safe_list = jnp.clip(owner_list, 0, REQ - 1)
    number_list = global_page - jnp.take(page_starts, safe_list)
    owner_list = jnp.where(live_page, safe_list, -1).astype(jnp.int32)
    number_list = jnp.where(live_page, number_list, 0).astype(jnp.int32)
    pair_order = jax.random.permutation(split_keys[3], half_count)
    heavy_pair = pair_order < max(1, seq_count // 4)
    heavy_side = jax.random.randint(split_keys[4], (half_count,), 0, 2)
    device_ids = jnp.arange(seq_count, dtype=jnp.int32)
    pair_index = device_ids % half_count
    upper_side = (device_ids >= half_count).astype(jnp.int32)
    heavy_device = jnp.take(heavy_pair, pair_index) & (jnp.take(heavy_side, pair_index) == upper_side)
    capacity = jnp.where(heavy_device, PAGES_DEV, PAGES_DEV // 2)
    slot_ids = jnp.arange(POOL, dtype=jnp.int32)
    allowed = slot_ids % PAGES_DEV < jnp.take(capacity, slot_ids // PAGES_DEV)
    heavy_slot = jnp.take(heavy_device, slot_ids // PAGES_DEV)
    slot_rank = jax.random.permutation(split_keys[5], POOL).astype(jnp.int32)
    order_key = jnp.where(allowed, jnp.where(heavy_slot, 0, POOL), 2 * POOL) + slot_rank
    slot_order = jnp.argsort(order_key)
    owners = jnp.full((POOL,), -1, jnp.int32).at[slot_order].set(owner_list)
    numbers = jnp.zeros((POOL,), jnp.int32).at[slot_order].set(number_list)
    return (lengths, owners, numbers)


def draw_lengths(key, part):
    return page_table(key)[0]


def draw_page_owner(key, part):
    return page_table(key)[1]


def draw_page_number(key, part):
    return page_table(key)[2]


def draw_key_pages(key, part):
    split_keys = jax.random.split(jax.random.fold_in(key, 11), 1)
    base_values = jax.random.truncated_normal(split_keys[0], -6.0, 6.0, (POOL, PAGE, D), jnp.float32)
    return base_values.astype(jnp.bfloat16)


def draw_alibi_slopes(key, part):
    split_keys = jax.random.split(jax.random.fold_in(key, 13), 3)
    slow_share = 0.5
    slow_head = jax.random.uniform(split_keys[0], (NH,), jnp.float32) < slow_share
    slow_rate = jnp.exp(jax.random.uniform(split_keys[1], (NH,), jnp.float32, math.log(0.2), math.log(2.0))) / MAXLEN
    fast_rate = jnp.exp(jax.random.uniform(split_keys[2], (NH,), jnp.float32, math.log(1.0 / 50.0), math.log(1.0 / 30.0)))
    return jnp.where(slow_head, slow_rate, fast_rate).astype(jnp.float32)


def block_scale(key, shape, pieces, smallest, largest):
    loudness = 1.0
    for position, blocks in pieces:
        heights = jax.random.uniform(jax.random.fold_in(jax.random.fold_in(key, 6), position), (blocks,), jnp.float32, smallest / len(pieces), largest / len(pieces))
        loudness = loudness * jnp.repeat(jnp.exp(heights), shape[position] // blocks).reshape((-1,) + (1,) * (len(shape) - 1 - position))
    return loudness


def noise(stream_key, shape, spread, bound, pieces=(), held_as=jnp.bfloat16):
    drawn = spread * jax.random.normal(stream_key, shape, jnp.float32)
    if pieces:
        drawn = drawn * block_scale(stream_key, shape, pieces, -0.22, 0.18)
    return jnp.clip(drawn, -bound, bound).astype(held_as)


def setup_inputs(seed: int = 0) -> dict:
    keys = jax.random.split(jax.random.key(seed), 14)
    tokens = noise(keys[0], (STEPS, REQ, D), 1.0, 6.0, ((2, 64),))
    lengths = draw_lengths(jax.random.fold_in(keys[13], 71), 0)
    page_owner = draw_page_owner(jax.random.fold_in(keys[13], 71), 0)
    page_number = draw_page_number(jax.random.fold_in(keys[13], 71), 0)
    key_pages = draw_key_pages(jax.random.fold_in(keys[13], 71), 0)
    value_pages = noise(keys[5], (POOL, PAGE, D), 1.0, 6.0, ((0, 64), (2, 4)))
    alibi_slopes = draw_alibi_slopes(jax.random.fold_in(keys[13], 71), 0)
    norm1_gain = jnp.clip(1.0 + 0.18 * jax.random.normal(keys[7], (D,), jnp.float32), 0.1, 1.9)
    norm2_gain = jnp.clip(1.0 + 0.18 * jax.random.normal(keys[8], (D,), jnp.float32), 0.1, 1.9)
    w_qkv = noise(keys[9], (D, 3, D), D ** -0.5, 0.09375, ((0, 64), (2, 4)))
    w_out = noise(keys[10], (D, D), D ** -0.5, 0.09375, ((0, 64), (1, 4)))
    w_up = noise(keys[11], (D, FF), D ** -0.5, 0.09375, ((0, 64), (1, 4)))
    w_down = noise(keys[12], (D, FF), FF ** -0.5, 0.046875, ((0, 64), (1, 4)))
    return {"tokens": tokens, "lengths": lengths, "page_owner": page_owner, "page_number": page_number, "key_pages": key_pages, "value_pages": value_pages, "alibi_slopes": alibi_slopes, "norm1_gain": norm1_gain, "norm2_gain": norm2_gain, "w_qkv": w_qkv, "w_out": w_out, "w_up": w_up, "w_down": w_down}


eps_norm = 1e-05
floor_score = -1e+30
highest = lax.Precision.HIGHEST

def normalize(token_rows, gain_full, width_all):
    token_float = token_rows.astype(jnp.float32)
    mean_value = lax.optimization_barrier(jnp.sum(token_float, axis=1)) / width_all
    variance = lax.optimization_barrier(jnp.sum(token_float * token_float, axis=1)) / width_all - mean_value * mean_value
    return ((token_float - mean_value[:, None]) * lax.rsqrt(variance + eps_norm)[:, None] * gain_full[None, :]).astype(jnp.bfloat16)

def page_block(carry_state, owners, number, key_block, value_block, queries, slopes, lengths, token_step):
    run_max, run_sum, run_out = carry_state
    nblock, page_len, width_all = key_block.shape
    nheads = slopes.shape[0]
    head_size = width_all // nheads
    requests = queries.shape[0]
    safe_owner = jnp.clip(owners, 0, requests - 1)
    page_query = jnp.take(queries, safe_owner, axis=0).astype(jnp.float32)
    key_heads = key_block.reshape(nblock, page_len, nheads, head_size).astype(jnp.float32)
    value_heads = value_block.reshape(nblock, page_len, nheads, head_size).astype(jnp.float32)
    scores = jnp.einsum('bhe,bthe->bth', page_query, key_heads) * head_size ** (-0.5)
    positions = number[:, None] * page_len + jnp.arange(page_len, dtype=jnp.int32)[None, :]
    own_length = jnp.take(lengths, safe_owner)
    distance = (own_length[:, None] + token_step - positions).astype(jnp.float32)
    scores = scores - distance[:, :, None] * slopes[None, None, :]
    valid_mask = (owners[:, None] >= 0) & (positions < own_length[:, None])
    masked = jnp.where(valid_mask[:, :, None], scores, floor_score)
    page_max = lax.optimization_barrier(jnp.max(masked, axis=1))
    member = owners[None, :] == jnp.arange(requests, dtype=jnp.int32)[:, None]
    block_max = lax.optimization_barrier(jnp.max(jnp.where(member[:, :, None], page_max[None, :, :], floor_score), axis=1))
    next_max = jnp.maximum(run_max, block_max)
    owner_max = jnp.take(next_max, safe_owner, axis=0)
    expon = jnp.where(valid_mask[:, :, None], jnp.exp(masked - owner_max[:, None, :]), 0.0)
    page_sum = lax.optimization_barrier(jnp.sum(expon, axis=1))
    weights = lax.optimization_barrier(expon.astype(jnp.bfloat16)).astype(jnp.float32)
    page_out = jnp.einsum('bth,bthe->bhe', weights, value_heads)
    member_float = member.astype(jnp.float32)
    rescale = jnp.exp(run_max - next_max)
    next_sum = run_sum * rescale + jnp.dot(member_float, page_sum, precision=highest)
    added = jnp.dot(member_float, page_out.reshape(nblock, nheads * head_size), precision=highest)
    next_out = run_out * rescale[:, :, None] + added.reshape(requests, nheads, head_size)
    return (next_max, next_sum, next_out)

def attend_new(carry_state, queries, new_keys, new_values, slopes, token_step):
    run_max, run_sum, run_out = carry_state
    head_size = queries.shape[2]
    for earlier in range(token_step + 1):
        scores = lax.optimization_barrier(jnp.sum(queries.astype(jnp.float32) * new_keys[earlier].astype(jnp.float32), axis=2)) * head_size ** (-0.5)
        scores = scores - slopes[None, :] * float(token_step - earlier)
        next_max = jnp.maximum(run_max, scores)
        rescale = jnp.exp(run_max - next_max)
        expon = jnp.exp(scores - next_max)
        weights = lax.optimization_barrier(expon.astype(jnp.bfloat16)).astype(jnp.float32)
        run_sum = run_sum * rescale + expon
        run_out = run_out * rescale[:, :, None] + weights[:, :, None] * new_values[earlier].astype(jnp.float32)
        run_max = next_max
    attended = (run_out / run_sum[:, :, None]).astype(jnp.bfloat16)
    return attended.reshape(attended.shape[0], -1)

def reference(tokens, lengths, page_owner, page_number, key_pages, value_pages, alibi_slopes, norm1_gain, norm2_gain, w_qkv, w_out, w_up, w_down):
    requests = tokens.shape[1]
    nblocks = POOL // BLK
    owner_blocks = page_owner.reshape(nblocks, BLK)
    number_blocks = page_number.reshape(nblocks, BLK)
    key_blocks = key_pages.reshape(nblocks, BLK, PAGE, D)
    value_blocks = value_pages.reshape(nblocks, BLK, PAGE, D)
    new_keys = []
    new_values = []
    outputs = []
    for token_step in range(STEPS):
        token_rows = tokens[token_step]
        token_float = token_rows.astype(jnp.float32)
        normed = normalize(token_rows, norm1_gain, D)
        joined = jnp.dot(normed, w_qkv.reshape(D, 3 * D), preferred_element_type=jnp.float32).astype(jnp.bfloat16)
        queries = joined[:, :D].reshape(requests, NH, HD)
        new_keys.append(joined[:, D:2 * D].reshape(requests, NH, HD))
        new_values.append(joined[:, 2 * D:].reshape(requests, NH, HD))
        initial = (jnp.full((requests, NH), floor_score, jnp.float32), jnp.zeros((requests, NH), jnp.float32), jnp.zeros((requests, NH, HD), jnp.float32))

        def page_step(carry_state, block_items):
            owners, number, key_block, value_block = block_items
            return (page_block(carry_state, owners, number, key_block, value_block, queries, alibi_slopes, lengths, token_step), None)
        final_state, _ = lax.scan(page_step, initial, (owner_blocks, number_blocks, key_blocks, value_blocks))
        attended = attend_new(final_state, queries, new_keys, new_values, alibi_slopes, token_step)
        projected = lax.dot_general(attended, w_out, (((1,), (1,)), ((), ())), preferred_element_type=jnp.float32)
        hidden_in = (token_float + projected).astype(jnp.bfloat16)
        hidden_float = hidden_in.astype(jnp.float32)
        normed_two = normalize(hidden_in, norm2_gain, D)
        up_proj = jnp.dot(normed_two, w_up, preferred_element_type=jnp.float32)
        hidden = jax.nn.gelu(up_proj, approximate=False).astype(jnp.bfloat16)
        down_proj = lax.dot_general(hidden, w_down, (((1,), (1,)), ((), ())), preferred_element_type=jnp.float32)
        outputs.append((hidden_float + down_proj).astype(jnp.bfloat16))
    return jnp.stack(outputs)
```

```python
import functools

import jax
import jax.numpy as jnp
from jax import lax
from jax.sharding import PartitionSpec as P

D = 4096
BLK = 8


eps_norm = 1e-05
floor_score = -1e30
highest = lax.Precision.HIGHEST


def normalize(token_rows, gain_share, totals, width_all):
    row_sum, row_squares = totals
    mean_value = row_sum / width_all
    variance = row_squares / width_all - mean_value * mean_value
    return (
        (token_rows.astype(jnp.float32) - mean_value[:, None])
        * lax.rsqrt(variance + eps_norm)[:, None]
        * gain_share[None, :]
    ).astype(jnp.bfloat16)


def page_block(
    carry_state, owners, number, key_block, value_block, queries, slopes, lengths, token_step
):
    run_max, run_sum, run_out = carry_state
    nblock, page_len, width_all = key_block.shape
    nheads = slopes.shape[0]
    head_size = width_all // nheads
    requests = queries.shape[0]
    safe_owner = jnp.clip(owners, 0, requests - 1)
    page_query = jnp.take(queries, safe_owner, axis=0)
    key_heads = key_block.reshape(nblock, page_len, nheads, head_size)
    value_heads = value_block.reshape(nblock, page_len, nheads, head_size)
    scores = jnp.einsum(
        "bhe,bthe->bth", page_query, key_heads, preferred_element_type=jnp.float32
    ) * head_size ** (-0.5)
    positions = number[:, None] * page_len + jnp.arange(page_len, dtype=jnp.int32)[None, :]
    own_length = jnp.take(lengths, safe_owner)
    distance = (own_length[:, None] + token_step - positions).astype(jnp.float32)
    scores = scores - distance[:, :, None] * slopes[None, None, :]
    valid_mask = (owners[:, None] >= 0) & (positions < own_length[:, None])
    masked = jnp.where(valid_mask[:, :, None], scores, floor_score)
    page_max = jnp.max(masked, axis=1)
    member = owners[None, :] == jnp.arange(requests, dtype=jnp.int32)[:, None]
    block_max = jnp.max(jnp.where(member[:, :, None], page_max[None, :, :], floor_score), axis=1)
    next_max = jnp.maximum(run_max, block_max)
    owner_max = jnp.take(next_max, safe_owner, axis=0)
    expon = jnp.where(valid_mask[:, :, None], jnp.exp(masked - owner_max[:, None, :]), 0.0)
    page_sum = jnp.sum(expon, axis=1)
    weights = expon.astype(jnp.bfloat16)
    page_out = jnp.einsum("bth,bthe->bhe", weights, value_heads, preferred_element_type=jnp.float32)
    member_float = member.astype(jnp.float32)
    rescale = jnp.exp(run_max - next_max)
    next_sum = run_sum * rescale + jnp.dot(member_float, page_sum, precision=highest)
    added = jnp.dot(member_float, page_out.reshape(nblock, nheads * head_size), precision=highest)
    next_out = run_out * rescale[:, :, None] + added.reshape(requests, nheads, head_size)
    return (next_max, next_sum, next_out)


def attend_new(carry_state, queries, new_keys, new_values, slopes, token_step):
    run_max, run_sum, run_out = carry_state
    head_size = queries.shape[2]
    for earlier in range(token_step + 1):
        scores = jnp.sum(
            queries.astype(jnp.float32) * new_keys[earlier].astype(jnp.float32), axis=2
        ) * head_size ** (-0.5)
        scores = scores - slopes[None, :] * float(token_step - earlier)
        next_max = jnp.maximum(run_max, scores)
        rescale = jnp.exp(run_max - next_max)
        expon = jnp.exp(scores - next_max)
        weights = lax.optimization_barrier(expon.astype(jnp.bfloat16)).astype(jnp.float32)
        run_sum = run_sum * rescale + expon
        run_out = run_out * rescale[:, :, None] + weights[:, :, None] * new_values[earlier].astype(
            jnp.float32
        )
        run_max = next_max
    attended = (run_out / run_sum[:, :, None]).astype(jnp.bfloat16)
    return attended.reshape(attended.shape[0], -1)


def gather_cols(part, axis_name):
    return lax.all_gather(part, axis_name, axis=1, tiled=True)


def full_normalize(rows, gain_full):
    row_float = rows.astype(jnp.float32)
    totals = (jnp.sum(row_float, axis=1), jnp.sum(row_float * row_float, axis=1))
    return normalize(rows, gain_full, totals, rows.shape[1])


def butterfly_combine(state, nseq):
    my_index = lax.axis_index("seq")
    stride = 1
    while stride < nseq:
        pairs = [(i, i ^ stride) for i in range(nseq)]
        other = lax.ppermute(state, "seq", pairs)
        low = (my_index & stride) == 0
        first = tuple(jnp.where(low, a, b) for a, b in zip(state, other))
        second = tuple(jnp.where(low, b, a) for a, b in zip(state, other))
        top = jnp.maximum(first[0], second[0])
        scale_a = jnp.exp(first[0] - top)
        scale_b = jnp.exp(second[0] - top)
        total = first[1] * scale_a + second[1] * scale_b
        out = first[2] * scale_a[:, :, None] + second[2] * scale_b[:, :, None]
        state = (top, total, out)
        stride *= 2
    return state


def on_device(
    tokens,
    lengths,
    page_owner,
    page_number,
    key_pages,
    value_pages,
    alibi_slopes,
    norm1_gain,
    norm2_gain,
    w_qkv,
    w_out,
    w_up,
    w_down,
    nseq,
):
    nsteps, requests, local_width = tokens.shape
    nheads = alibi_slopes.shape[0]
    head_width = key_pages.shape[2]
    head_size = head_width // nheads
    nblocks = key_pages.shape[0] // BLK
    qkv_width = w_qkv.shape[1] * w_qkv.shape[2]
    rows = nsteps * requests

    qkv_cols = lax.all_to_all(w_qkv.reshape(local_width, qkv_width), "seq", 1, 0, tiled=True)
    up_cols = lax.all_to_all(w_up, "seq", 1, 0, tiled=True)
    gains = lax.all_gather(jnp.stack([norm1_gain, norm2_gain]), "seq", axis=1, tiled=True)

    token_rows = tokens.reshape(rows, local_width)
    token_float = token_rows.astype(jnp.float32)
    normed = full_normalize(gather_cols(token_rows, "seq"), gains[0])
    qkv_part = jnp.dot(normed, qkv_cols, preferred_element_type=jnp.float32).astype(jnp.bfloat16)
    joined = gather_cols(qkv_part, "seq")
    all_queries = joined[:, :head_width].reshape(nsteps, requests, nheads, head_size)
    new_keys = joined[:, head_width : 2 * head_width].reshape(nsteps, requests, nheads, head_size)
    new_values = joined[:, 2 * head_width :].reshape(nsteps, requests, nheads, head_size)

    states = []
    for token_step in range(nsteps):
        queries = all_queries[token_step]
        carry_state = (
            jnp.full((requests, nheads), floor_score, jnp.float32),
            jnp.zeros((requests, nheads), jnp.float32),
            jnp.zeros((requests, nheads, head_size), jnp.float32),
        )

        def visit(turn_index, state_in):
            first_page = (turn_index * BLK).astype(jnp.int32)
            owners = lax.dynamic_slice_in_dim(page_owner, first_page, BLK, 0)
            number = lax.dynamic_slice_in_dim(page_number, first_page, BLK, 0)
            key_block = lax.dynamic_slice_in_dim(key_pages, first_page, BLK, 0)
            value_block = lax.dynamic_slice_in_dim(value_pages, first_page, BLK, 0)

            def compute(state_given):
                return page_block(
                    state_given,
                    owners,
                    number,
                    key_block,
                    value_block,
                    queries,
                    alibi_slopes,
                    lengths,
                    token_step,
                )

            def keep_state(state_given):
                return state_given

            return lax.cond(jnp.any(owners >= 0), compute, keep_state, state_in)

        states.append(lax.fori_loop(0, nblocks, visit, carry_state))

    joined_state = tuple(jnp.concatenate(parts, axis=0) for parts in zip(*states))
    run_max, run_sum, run_out = butterfly_combine(joined_state, nseq)
    attended = []
    for token_step in range(nsteps):
        picked = slice(token_step * requests, (token_step + 1) * requests)
        attended.append(
            attend_new(
                (run_max[picked], run_sum[picked], run_out[picked]),
                all_queries[token_step],
                new_keys,
                new_values,
                alibi_slopes,
                token_step,
            )
        )
    attended = jnp.concatenate(attended, axis=0)
    projected = lax.psum(
        lax.dot_general(attended, w_out, (((1,), (1,)), ((), ())), preferred_element_type=jnp.float32),
        "head",
    )
    hidden_in = (token_float + projected).astype(jnp.bfloat16)
    hidden_float = hidden_in.astype(jnp.float32)
    normed_two = full_normalize(gather_cols(hidden_in, "seq"), gains[1])
    up_share = jnp.dot(normed_two, up_cols, preferred_element_type=jnp.float32)
    hidden_share = jax.nn.gelu(up_share, approximate=False).astype(jnp.bfloat16)
    down_part = lax.dot_general(
        gather_cols(hidden_share, "seq"),
        w_down,
        (((1,), (1,)), ((), ())),
        preferred_element_type=jnp.float32,
    )
    down_proj = lax.psum(down_part, "head")
    return (hidden_float + down_proj).astype(jnp.bfloat16).reshape(nsteps, requests, local_width)


def solution(mesh):
    placed = (
        P(None, None, "seq"),
        P(),
        P("seq"),
        P("seq"),
        P("seq", None, "head"),
        P("seq", None, "head"),
        P("head"),
        P("seq"),
        P("seq"),
        P("seq", None, "head"),
        P("seq", "head"),
        P("seq", "head"),
        P("seq", "head"),
    )
    nseq = mesh.shape["seq"]
    return jax.shard_map(
        functools.partial(on_device, nseq=nseq), mesh=mesh, in_specs=placed, out_specs=P(None, None, "seq"), check_vma=False
    )
```

```python
import functools

import jax
import jax.numpy as jnp
from jax import lax
from jax.sharding import PartitionSpec as P

D = 4096
BLK = 8


eps_norm = 1e-05
floor_score = -1e30
highest = lax.Precision.HIGHEST


def normalize(token_rows, gain_share, totals, width_all):
    row_sum, row_squares = totals
    mean_value = row_sum / width_all
    variance = row_squares / width_all - mean_value * mean_value
    return (
        (token_rows.astype(jnp.float32) - mean_value[:, None])
        * lax.rsqrt(variance + eps_norm)[:, None]
        * gain_share[None, :]
    ).astype(jnp.bfloat16)


def page_block(
    carry_state, owners, number, key_block, value_block, queries, slopes, lengths, token_step
):
    run_max, run_sum, run_out = carry_state
    nblock, page_len, width_all = key_block.shape
    nheads = slopes.shape[0]
    head_size = width_all // nheads
    requests = queries.shape[0]
    safe_owner = jnp.clip(owners, 0, requests - 1)
    page_query = jnp.take(queries, safe_owner, axis=0)
    key_heads = key_block.reshape(nblock, page_len, nheads, head_size)
    value_heads = value_block.reshape(nblock, page_len, nheads, head_size)
    scores = jnp.einsum(
        "bhe,bthe->bth", page_query, key_heads, preferred_element_type=jnp.float32
    ) * head_size ** (-0.5)
    positions = number[:, None] * page_len + jnp.arange(page_len, dtype=jnp.int32)[None, :]
    own_length = jnp.take(lengths, safe_owner)
    distance = (own_length[:, None] + token_step - positions).astype(jnp.float32)
    scores = scores - distance[:, :, None] * slopes[None, None, :]
    valid_mask = (owners[:, None] >= 0) & (positions < own_length[:, None])
    masked = jnp.where(valid_mask[:, :, None], scores, floor_score)
    page_max = jnp.max(masked, axis=1)
    member = owners[None, :] == jnp.arange(requests, dtype=jnp.int32)[:, None]
    block_max = jnp.max(jnp.where(member[:, :, None], page_max[None, :, :], floor_score), axis=1)
    next_max = jnp.maximum(run_max, block_max)
    owner_max = jnp.take(next_max, safe_owner, axis=0)
    expon = jnp.where(valid_mask[:, :, None], jnp.exp(masked - owner_max[:, None, :]), 0.0)
    page_sum = jnp.sum(expon, axis=1)
    weights = expon.astype(jnp.bfloat16)
    page_out = jnp.einsum("bth,bthe->bhe", weights, value_heads, preferred_element_type=jnp.float32)
    member_float = member.astype(jnp.float32)
    rescale = jnp.exp(run_max - next_max)
    next_sum = run_sum * rescale + jnp.dot(member_float, page_sum, precision=highest)
    added = jnp.dot(member_float, page_out.reshape(nblock, nheads * head_size), precision=highest)
    next_out = run_out * rescale[:, :, None] + added.reshape(requests, nheads, head_size)
    return (next_max, next_sum, next_out)


def attend_new(carry_state, queries, new_keys, new_values, slopes, token_step):
    run_max, run_sum, run_out = carry_state
    head_size = queries.shape[2]
    for earlier in range(token_step + 1):
        scores = jnp.sum(
            queries.astype(jnp.float32) * new_keys[earlier].astype(jnp.float32), axis=2
        ) * head_size ** (-0.5)
        scores = scores - slopes[None, :] * float(token_step - earlier)
        next_max = jnp.maximum(run_max, scores)
        rescale = jnp.exp(run_max - next_max)
        expon = jnp.exp(scores - next_max)
        weights = lax.optimization_barrier(expon.astype(jnp.bfloat16)).astype(jnp.float32)
        run_sum = run_sum * rescale + expon
        run_out = run_out * rescale[:, :, None] + weights[:, :, None] * new_values[earlier].astype(
            jnp.float32
        )
        run_max = next_max
    attended = (run_out / run_sum[:, :, None]).astype(jnp.bfloat16)
    return attended.reshape(attended.shape[0], -1)


def gather_cols(part, axis_name):
    return lax.all_gather(part, axis_name, axis=1, tiled=True)


def full_normalize(rows, gain_full):
    row_float = rows.astype(jnp.float32)
    totals = (jnp.sum(row_float, axis=1), jnp.sum(row_float * row_float, axis=1))
    return normalize(rows, gain_full, totals, rows.shape[1])


def butterfly_combine(state, nseq):
    my_index = lax.axis_index("seq")
    stride = 1
    while stride < nseq:
        pairs = [(i, i ^ stride) for i in range(nseq)]
        other = lax.ppermute(state, "seq", pairs)
        low = (my_index & stride) == 0
        first = tuple(jnp.where(low, a, b) for a, b in zip(state, other))
        second = tuple(jnp.where(low, b, a) for a, b in zip(state, other))
        top = jnp.maximum(first[0], second[0])
        scale_a = jnp.exp(first[0] - top)
        scale_b = jnp.exp(second[0] - top)
        total = first[1] * scale_a + second[1] * scale_b
        out = first[2] * scale_a[:, :, None] + second[2] * scale_b[:, :, None]
        state = (top, total, out)
        stride *= 2
    return state


def attend_rows(carry_state, queries, new_keys, new_values, slopes, token_step):
    run_max, run_sum, run_out = carry_state
    head_size = queries.shape[2]
    for earlier in range(len(new_keys)):
        active = earlier <= token_step
        scores = jnp.sum(
            queries.astype(jnp.float32) * new_keys[earlier].astype(jnp.float32), axis=2
        ) * head_size ** (-0.5)
        scores = scores - slopes[None, :] * (token_step - earlier).astype(jnp.float32)
        next_max = jnp.maximum(run_max, scores)
        rescale = jnp.exp(run_max - next_max)
        expon = jnp.exp(scores - next_max)
        weights = lax.optimization_barrier(expon.astype(jnp.bfloat16)).astype(jnp.float32)
        next_sum = run_sum * rescale + expon
        next_out = run_out * rescale[:, :, None] + weights[:, :, None] * new_values[earlier].astype(
            jnp.float32
        )
        run_sum = jnp.where(active, next_sum, run_sum)
        run_out = jnp.where(active, next_out, run_out)
        run_max = jnp.where(active, next_max, run_max)
    attended = (run_out / run_sum[:, :, None]).astype(jnp.bfloat16)
    return attended.reshape(attended.shape[0], -1)


def on_device(
    tokens,
    lengths,
    page_owner,
    page_number,
    key_pages,
    value_pages,
    alibi_slopes,
    norm1_gain,
    norm2_gain,
    w_qkv,
    w_out,
    w_up,
    w_down,
    nseq,
):
    nsteps, requests, local_width = tokens.shape
    nheads = alibi_slopes.shape[0]
    head_width = key_pages.shape[2]
    head_size = head_width // nheads
    nblocks = key_pages.shape[0] // BLK
    qkv_width = w_qkv.shape[1] * w_qkv.shape[2]
    rows = nsteps * requests

    qkv_chunk = qkv_width // nseq
    up_chunk = w_up.shape[1] // nseq
    both = jnp.concatenate(
        [
            w_qkv.reshape(local_width, nseq, qkv_chunk),
            w_up.reshape(local_width, nseq, up_chunk),
        ],
        axis=2,
    )
    both = lax.all_to_all(both, "seq", 1, 0, tiled=True).reshape(nseq * local_width, qkv_chunk + up_chunk)
    qkv_cols = both[:, :qkv_chunk]
    up_cols = both[:, qkv_chunk:]
    gains = lax.all_gather(jnp.stack([norm1_gain, norm2_gain]), "seq", axis=1, tiled=True)

    token_rows = tokens.reshape(rows, local_width)
    token_float = token_rows.astype(jnp.float32)
    normed = full_normalize(gather_cols(token_rows, "seq"), gains[0])
    qkv_part = jnp.dot(normed, qkv_cols, preferred_element_type=jnp.float32).astype(jnp.bfloat16)
    joined = gather_cols(qkv_part, "seq")
    all_queries = joined[:, :head_width].reshape(nsteps, requests, nheads, head_size)
    new_keys = joined[:, head_width : 2 * head_width].reshape(nsteps, requests, nheads, head_size)
    new_values = joined[:, 2 * head_width :].reshape(nsteps, requests, nheads, head_size)

    states = []
    for token_step in range(nsteps):
        queries = all_queries[token_step]
        carry_state = (
            jnp.full((requests, nheads), floor_score, jnp.float32),
            jnp.zeros((requests, nheads), jnp.float32),
            jnp.zeros((requests, nheads, head_size), jnp.float32),
        )

        def visit(turn_index, state_in):
            first_page = (turn_index * BLK).astype(jnp.int32)
            owners = lax.dynamic_slice_in_dim(page_owner, first_page, BLK, 0)
            number = lax.dynamic_slice_in_dim(page_number, first_page, BLK, 0)
            key_block = lax.dynamic_slice_in_dim(key_pages, first_page, BLK, 0)
            value_block = lax.dynamic_slice_in_dim(value_pages, first_page, BLK, 0)

            def compute(state_given):
                return page_block(
                    state_given,
                    owners,
                    number,
                    key_block,
                    value_block,
                    queries,
                    alibi_slopes,
                    lengths,
                    token_step,
                )

            def keep_state(state_given):
                return state_given

            return lax.cond(jnp.any(owners >= 0), compute, keep_state, state_in)

        states.append(lax.fori_loop(0, nblocks, visit, carry_state))

    run_max, run_sum, run_out = (jnp.concatenate(parts, axis=0) for parts in zip(*states))
    packed = jnp.concatenate([run_out, run_max[:, :, None], run_sum[:, :, None]], axis=2)
    own_rows = rows // nseq
    packed = lax.all_to_all(
        packed.reshape(nseq, own_rows, nheads, head_size + 2), "seq", 0, 0, tiled=True
    )
    part_out = packed[:, :, :, :head_size]
    part_max = packed[:, :, :, head_size]
    part_sum = packed[:, :, :, head_size + 1]
    top_max = jnp.max(part_max, axis=0)
    rescale = jnp.exp(part_max - top_max[None])
    top_sum = jnp.sum(part_sum * rescale, axis=0)
    top_out = jnp.sum(part_out * rescale[:, :, :, None], axis=0)
    first_row = lax.axis_index("seq") * own_rows
    my_step = first_row // requests
    pick = lambda a: lax.dynamic_slice_in_dim(a.reshape(rows, nheads, head_size), first_row, own_rows, 0)
    my_queries = pick(all_queries)
    my_keys = []
    my_values = []
    for earlier in range(nsteps):
        shifted = first_row - (my_step - earlier) * requests
        my_keys.append(lax.dynamic_slice_in_dim(new_keys.reshape(rows, nheads, head_size), shifted, own_rows, 0))
        my_values.append(lax.dynamic_slice_in_dim(new_values.reshape(rows, nheads, head_size), shifted, own_rows, 0))
    mine = attend_rows(
        (top_max, top_sum, top_out), my_queries, my_keys, my_values, alibi_slopes, my_step
    )
    attended = lax.all_gather(mine, "seq", axis=0, tiled=True)
    projected = lax.psum(
        lax.dot_general(attended, w_out, (((1,), (1,)), ((), ())), preferred_element_type=jnp.float32),
        "head",
    )
    hidden_in = (token_float + projected).astype(jnp.bfloat16)
    hidden_float = hidden_in.astype(jnp.float32)
    normed_two = full_normalize(gather_cols(hidden_in, "seq"), gains[1])
    up_share = jnp.dot(normed_two, up_cols, preferred_element_type=jnp.float32)
    hidden_share = jax.nn.gelu(up_share, approximate=False).astype(jnp.bfloat16)
    down_part = lax.dot_general(
        gather_cols(hidden_share, "seq"),
        w_down,
        (((1,), (1,)), ((), ())),
        preferred_element_type=jnp.float32,
    )
    down_proj = lax.psum(down_part, "head")
    return (hidden_float + down_proj).astype(jnp.bfloat16).reshape(nsteps, requests, local_width)


def solution(mesh):
    placed = (
        P(None, None, "seq"),
        P(),
        P("seq"),
        P("seq"),
        P("seq", None, "head"),
        P("seq", None, "head"),
        P("head"),
        P("seq"),
        P("seq"),
        P("seq", None, "head"),
        P("seq", "head"),
        P("seq", "head"),
        P("seq", "head"),
    )
    nseq = mesh.shape["seq"]
    return jax.shard_map(
        functools.partial(on_device, nseq=nseq), mesh=mesh, in_specs=placed, out_specs=P(None, None, "seq"), check_vma=False
    )
```

```python
import functools

import jax
import jax.numpy as jnp
from jax import lax
from jax.sharding import PartitionSpec as P

D = 4096
BLK = 8


eps_norm = 1e-05
floor_score = -1e30
highest = lax.Precision.HIGHEST


def normalize(token_rows, gain_share, totals, width_all):
    row_sum, row_squares = totals
    mean_value = row_sum / width_all
    variance = row_squares / width_all - mean_value * mean_value
    return (
        (token_rows.astype(jnp.float32) - mean_value[:, None])
        * lax.rsqrt(variance + eps_norm)[:, None]
        * gain_share[None, :]
    ).astype(jnp.bfloat16)


def page_block(
    carry_state, owners, number, key_block, value_block, queries, slopes, lengths, token_step
):
    run_max, run_sum, run_out = carry_state
    nblock, page_len, width_all = key_block.shape
    nheads = slopes.shape[0]
    head_size = width_all // nheads
    requests = queries.shape[0]
    safe_owner = jnp.clip(owners, 0, requests - 1)
    page_query = jnp.take(queries, safe_owner, axis=0)
    key_heads = key_block.reshape(nblock, page_len, nheads, head_size)
    value_heads = value_block.reshape(nblock, page_len, nheads, head_size)
    scores = jnp.einsum(
        "bhe,bthe->bth", page_query, key_heads, preferred_element_type=jnp.float32
    ) * head_size ** (-0.5)
    positions = number[:, None] * page_len + jnp.arange(page_len, dtype=jnp.int32)[None, :]
    own_length = jnp.take(lengths, safe_owner)
    distance = (own_length[:, None] + token_step - positions).astype(jnp.float32)
    scores = scores - distance[:, :, None] * slopes[None, None, :]
    valid_mask = (owners[:, None] >= 0) & (positions < own_length[:, None])
    masked = jnp.where(valid_mask[:, :, None], scores, floor_score)
    page_max = jnp.max(masked, axis=1)
    member = owners[None, :] == jnp.arange(requests, dtype=jnp.int32)[:, None]
    block_max = jnp.max(jnp.where(member[:, :, None], page_max[None, :, :], floor_score), axis=1)
    next_max = jnp.maximum(run_max, block_max)
    owner_max = jnp.take(next_max, safe_owner, axis=0)
    expon = jnp.where(valid_mask[:, :, None], jnp.exp(masked - owner_max[:, None, :]), 0.0)
    page_sum = jnp.sum(expon, axis=1)
    weights = expon.astype(jnp.bfloat16)
    page_out = jnp.einsum("bth,bthe->bhe", weights, value_heads, preferred_element_type=jnp.float32)
    member_float = member.astype(jnp.float32)
    rescale = jnp.exp(run_max - next_max)
    next_sum = run_sum * rescale + jnp.dot(member_float, page_sum, precision=highest)
    added = jnp.dot(member_float, page_out.reshape(nblock, nheads * head_size), precision=highest)
    next_out = run_out * rescale[:, :, None] + added.reshape(requests, nheads, head_size)
    return (next_max, next_sum, next_out)


def attend_new(carry_state, queries, new_keys, new_values, slopes, token_step):
    run_max, run_sum, run_out = carry_state
    head_size = queries.shape[2]
    for earlier in range(token_step + 1):
        scores = jnp.sum(
            queries.astype(jnp.float32) * new_keys[earlier].astype(jnp.float32), axis=2
        ) * head_size ** (-0.5)
        scores = scores - slopes[None, :] * float(token_step - earlier)
        next_max = jnp.maximum(run_max, scores)
        rescale = jnp.exp(run_max - next_max)
        expon = jnp.exp(scores - next_max)
        weights = lax.optimization_barrier(expon.astype(jnp.bfloat16)).astype(jnp.float32)
        run_sum = run_sum * rescale + expon
        run_out = run_out * rescale[:, :, None] + weights[:, :, None] * new_values[earlier].astype(
            jnp.float32
        )
        run_max = next_max
    attended = (run_out / run_sum[:, :, None]).astype(jnp.bfloat16)
    return attended.reshape(attended.shape[0], -1)


def gather_rows(part, nseq):
    copies = jnp.broadcast_to(part[None], (nseq,) + part.shape)
    return lax.all_to_all(copies, "seq", 0, 0, tiled=True)


def gather_cols(part, nseq):
    got = gather_rows(part, nseq)
    return jnp.moveaxis(got, 0, -2).reshape(part.shape[:-1] + (nseq * part.shape[-1],))


def head_sum(part, nhead):
    my_index = lax.axis_index("head")
    stride = 1
    while stride < nhead:
        other = lax.ppermute(part, "head", [(i, i ^ stride) for i in range(nhead)])
        low = (my_index & stride) == 0
        part = jnp.where(low, part + other, other + part)
        stride *= 2
    return part


def full_normalize(rows, gain_full):
    row_float = rows.astype(jnp.float32)
    totals = (jnp.sum(row_float, axis=1), jnp.sum(row_float * row_float, axis=1))
    return normalize(rows, gain_full, totals, rows.shape[1])


def butterfly_combine(state, nseq):
    my_index = lax.axis_index("seq")
    stride = 1
    while stride < nseq:
        pairs = [(i, i ^ stride) for i in range(nseq)]
        other = lax.ppermute(state, "seq", pairs)
        low = (my_index & stride) == 0
        first = tuple(jnp.where(low, a, b) for a, b in zip(state, other))
        second = tuple(jnp.where(low, b, a) for a, b in zip(state, other))
        top = jnp.maximum(first[0], second[0])
        scale_a = jnp.exp(first[0] - top)
        scale_b = jnp.exp(second[0] - top)
        total = first[1] * scale_a + second[1] * scale_b
        out = first[2] * scale_a[:, :, None] + second[2] * scale_b[:, :, None]
        state = (top, total, out)
        stride *= 2
    return state


def attend_rows(carry_state, queries, new_keys, new_values, slopes, token_step):
    run_max, run_sum, run_out = carry_state
    head_size = queries.shape[2]
    for earlier in range(len(new_keys)):
        active = earlier <= token_step
        scores = jnp.sum(
            queries.astype(jnp.float32) * new_keys[earlier].astype(jnp.float32), axis=2
        ) * head_size ** (-0.5)
        scores = scores - slopes[None, :] * (token_step - earlier).astype(jnp.float32)
        next_max = jnp.maximum(run_max, scores)
        rescale = jnp.exp(run_max - next_max)
        expon = jnp.exp(scores - next_max)
        weights = lax.optimization_barrier(expon.astype(jnp.bfloat16)).astype(jnp.float32)
        next_sum = run_sum * rescale + expon
        next_out = run_out * rescale[:, :, None] + weights[:, :, None] * new_values[earlier].astype(
            jnp.float32
        )
        run_sum = jnp.where(active, next_sum, run_sum)
        run_out = jnp.where(active, next_out, run_out)
        run_max = jnp.where(active, next_max, run_max)
    attended = (run_out / run_sum[:, :, None]).astype(jnp.bfloat16)
    return attended.reshape(attended.shape[0], -1)


def on_device(
    tokens,
    lengths,
    page_owner,
    page_number,
    key_pages,
    value_pages,
    alibi_slopes,
    norm1_gain,
    norm2_gain,
    w_qkv,
    w_out,
    w_up,
    w_down,
    nseq,
    nhead,
):
    nsteps, requests, local_width = tokens.shape
    nheads = alibi_slopes.shape[0]
    head_width = key_pages.shape[2]
    head_size = head_width // nheads
    nblocks = key_pages.shape[0] // BLK
    qkv_width = w_qkv.shape[1] * w_qkv.shape[2]
    rows = nsteps * requests

    qkv_chunk = qkv_width // nseq
    up_chunk = w_up.shape[1] // nseq
    both = jnp.concatenate(
        [
            w_qkv.reshape(local_width, nseq, qkv_chunk),
            w_up.reshape(local_width, nseq, up_chunk),
        ],
        axis=2,
    )
    both = lax.all_to_all(both, "seq", 1, 0, tiled=True).reshape(nseq * local_width, qkv_chunk + up_chunk)
    qkv_cols = both[:, :qkv_chunk]
    up_cols = both[:, qkv_chunk:]
    gains = gather_cols(jnp.stack([norm1_gain, norm2_gain]), nseq)

    token_rows = tokens.reshape(rows, local_width)
    token_float = token_rows.astype(jnp.float32)
    normed = full_normalize(gather_cols(token_rows, nseq), gains[0])
    qkv_part = jnp.dot(normed, qkv_cols, preferred_element_type=jnp.float32).astype(jnp.bfloat16)
    joined = gather_cols(qkv_part, nseq)
    all_queries = joined[:, :head_width].reshape(nsteps, requests, nheads, head_size)
    new_keys = joined[:, head_width : 2 * head_width].reshape(nsteps, requests, nheads, head_size)
    new_values = joined[:, 2 * head_width :].reshape(nsteps, requests, nheads, head_size)

    states = []
    for token_step in range(nsteps):
        queries = all_queries[token_step]
        carry_state = (
            jnp.full((requests, nheads), floor_score, jnp.float32),
            jnp.zeros((requests, nheads), jnp.float32),
            jnp.zeros((requests, nheads, head_size), jnp.float32),
        )

        def visit(turn_index, state_in):
            first_page = (turn_index * BLK).astype(jnp.int32)
            owners = lax.dynamic_slice_in_dim(page_owner, first_page, BLK, 0)
            number = lax.dynamic_slice_in_dim(page_number, first_page, BLK, 0)
            key_block = lax.dynamic_slice_in_dim(key_pages, first_page, BLK, 0)
            value_block = lax.dynamic_slice_in_dim(value_pages, first_page, BLK, 0)

            def compute(state_given):
                return page_block(
                    state_given,
                    owners,
                    number,
                    key_block,
                    value_block,
                    queries,
                    alibi_slopes,
                    lengths,
                    token_step,
                )

            def keep_state(state_given):
                return state_given

            return lax.cond(jnp.any(owners >= 0), compute, keep_state, state_in)

        states.append(lax.fori_loop(0, nblocks, visit, carry_state))

    run_max, run_sum, run_out = (jnp.concatenate(parts, axis=0) for parts in zip(*states))
    packed = jnp.concatenate([run_out, run_max[:, :, None], run_sum[:, :, None]], axis=2)
    own_rows = rows // nseq
    packed = lax.all_to_all(
        packed.reshape(nseq, own_rows, nheads, head_size + 2), "seq", 0, 0, tiled=True
    )
    part_out = packed[:, :, :, :head_size]
    part_max = packed[:, :, :, head_size]
    part_sum = packed[:, :, :, head_size + 1]
    top_max = jnp.max(part_max, axis=0)
    rescale = jnp.exp(part_max - top_max[None])
    top_sum = jnp.sum(part_sum * rescale, axis=0)
    top_out = jnp.sum(part_out * rescale[:, :, :, None], axis=0)
    first_row = lax.axis_index("seq") * own_rows
    my_step = first_row // requests
    pick = lambda a: lax.dynamic_slice_in_dim(a.reshape(rows, nheads, head_size), first_row, own_rows, 0)
    my_queries = pick(all_queries)
    my_keys = []
    my_values = []
    for earlier in range(nsteps):
        shifted = first_row - (my_step - earlier) * requests
        my_keys.append(lax.dynamic_slice_in_dim(new_keys.reshape(rows, nheads, head_size), shifted, own_rows, 0))
        my_values.append(lax.dynamic_slice_in_dim(new_values.reshape(rows, nheads, head_size), shifted, own_rows, 0))
    mine = attend_rows(
        (top_max, top_sum, top_out), my_queries, my_keys, my_values, alibi_slopes, my_step
    )
    attended = gather_rows(mine, nseq).reshape(rows, -1)
    projected = head_sum(
        lax.dot_general(attended, w_out, (((1,), (1,)), ((), ())), preferred_element_type=jnp.float32),
        nhead,
    )
    hidden_in = (token_float + projected).astype(jnp.bfloat16)
    hidden_float = hidden_in.astype(jnp.float32)
    normed_two = full_normalize(gather_cols(hidden_in, nseq), gains[1])
    up_share = jnp.dot(normed_two, up_cols, preferred_element_type=jnp.float32)
    hidden_share = jax.nn.gelu(up_share, approximate=False).astype(jnp.bfloat16)
    down_part = lax.dot_general(
        gather_cols(hidden_share, nseq),
        w_down,
        (((1,), (1,)), ((), ())),
        preferred_element_type=jnp.float32,
    )
    down_proj = head_sum(down_part, nhead)
    return (hidden_float + down_proj).astype(jnp.bfloat16).reshape(nsteps, requests, local_width)


def solution(mesh):
    placed = (
        P(None, None, "seq"),
        P(),
        P("seq"),
        P("seq"),
        P("seq", None, "head"),
        P("seq", None, "head"),
        P("head"),
        P("seq"),
        P("seq"),
        P("seq", None, "head"),
        P("seq", "head"),
        P("seq", "head"),
        P("seq", "head"),
    )
    nseq = mesh.shape["seq"]
    return jax.shard_map(
        functools.partial(on_device, nseq=nseq, nhead=mesh.shape["head"]), mesh=mesh, in_specs=placed, out_specs=P(None, None, "seq"), check_vma=False
    )
```

```python
import functools

import jax
import jax.numpy as jnp
from jax import lax
from jax.sharding import PartitionSpec as P

D = 4096
BLK = 8


eps_norm = 1e-05
floor_score = -1e30
highest = lax.Precision.HIGHEST


def normalize(token_rows, gain_share, totals, width_all):
    row_sum, row_squares = totals
    mean_value = row_sum / width_all
    variance = row_squares / width_all - mean_value * mean_value
    return (
        (token_rows.astype(jnp.float32) - mean_value[:, None])
        * lax.rsqrt(variance + eps_norm)[:, None]
        * gain_share[None, :]
    ).astype(jnp.bfloat16)


def page_block(
    carry_state, owners, number, key_block, value_block, queries, slopes, lengths, token_step
):
    run_max, run_sum, run_out = carry_state
    nblock, page_len, width_all = key_block.shape
    nheads = slopes.shape[0]
    head_size = width_all // nheads
    requests = queries.shape[0]
    safe_owner = jnp.clip(owners, 0, requests - 1)
    page_query = jnp.take(queries, safe_owner, axis=0)
    key_heads = key_block.reshape(nblock, page_len, nheads, head_size)
    value_heads = value_block.reshape(nblock, page_len, nheads, head_size)
    scores = jnp.einsum(
        "bhe,bthe->bth", page_query, key_heads, preferred_element_type=jnp.float32
    ) * head_size ** (-0.5)
    positions = number[:, None] * page_len + jnp.arange(page_len, dtype=jnp.int32)[None, :]
    own_length = jnp.take(lengths, safe_owner)
    distance = (own_length[:, None] + token_step - positions).astype(jnp.float32)
    scores = scores - distance[:, :, None] * slopes[None, None, :]
    valid_mask = (owners[:, None] >= 0) & (positions < own_length[:, None])
    masked = jnp.where(valid_mask[:, :, None], scores, floor_score)
    page_max = jnp.max(masked, axis=1)
    member = owners[None, :] == jnp.arange(requests, dtype=jnp.int32)[:, None]
    block_max = jnp.max(jnp.where(member[:, :, None], page_max[None, :, :], floor_score), axis=1)
    next_max = jnp.maximum(run_max, block_max)
    owner_max = jnp.take(next_max, safe_owner, axis=0)
    expon = jnp.where(valid_mask[:, :, None], jnp.exp(masked - owner_max[:, None, :]), 0.0)
    page_sum = jnp.sum(expon, axis=1)
    weights = expon.astype(jnp.bfloat16)
    page_out = jnp.einsum("bth,bthe->bhe", weights, value_heads, preferred_element_type=jnp.float32)
    member_float = member.astype(jnp.float32)
    rescale = jnp.exp(run_max - next_max)
    next_sum = run_sum * rescale + jnp.dot(member_float, page_sum, precision=highest)
    added = jnp.dot(member_float, page_out.reshape(nblock, nheads * head_size), precision=highest)
    next_out = run_out * rescale[:, :, None] + added.reshape(requests, nheads, head_size)
    return (next_max, next_sum, next_out)


def attend_new(carry_state, queries, new_keys, new_values, slopes, token_step):
    run_max, run_sum, run_out = carry_state
    head_size = queries.shape[2]
    for earlier in range(token_step + 1):
        scores = jnp.sum(
            queries.astype(jnp.float32) * new_keys[earlier].astype(jnp.float32), axis=2
        ) * head_size ** (-0.5)
        scores = scores - slopes[None, :] * float(token_step - earlier)
        next_max = jnp.maximum(run_max, scores)
        rescale = jnp.exp(run_max - next_max)
        expon = jnp.exp(scores - next_max)
        weights = lax.optimization_barrier(expon.astype(jnp.bfloat16)).astype(jnp.float32)
        run_sum = run_sum * rescale + expon
        run_out = run_out * rescale[:, :, None] + weights[:, :, None] * new_values[earlier].astype(
            jnp.float32
        )
        run_max = next_max
    attended = (run_out / run_sum[:, :, None]).astype(jnp.bfloat16)
    return attended.reshape(attended.shape[0], -1)


def gather_rows(part, nseq):
    copies = jnp.broadcast_to(part[None], (nseq,) + part.shape)
    return lax.all_to_all(copies, "seq", 0, 0, tiled=True)


def gather_cols(part, nseq):
    got = gather_rows(part, nseq)
    return jnp.moveaxis(got, 0, -2).reshape(part.shape[:-1] + (nseq * part.shape[-1],))


def head_sum(part, nhead):
    my_index = lax.axis_index("head")
    stride = 1
    while stride < nhead:
        other = lax.ppermute(part, "head", [(i, i ^ stride) for i in range(nhead)])
        low = (my_index & stride) == 0
        part = jnp.where(low, part + other, other + part)
        stride *= 2
    return part


def full_normalize(rows, gain_full):
    row_float = rows.astype(jnp.float32)
    totals = (jnp.sum(row_float, axis=1), jnp.sum(row_float * row_float, axis=1))
    return normalize(rows, gain_full, totals, rows.shape[1])


def butterfly_combine(state, nseq):
    my_index = lax.axis_index("seq")
    stride = 1
    while stride < nseq:
        pairs = [(i, i ^ stride) for i in range(nseq)]
        other = lax.ppermute(state, "seq", pairs)
        low = (my_index & stride) == 0
        first = tuple(jnp.where(low, a, b) for a, b in zip(state, other))
        second = tuple(jnp.where(low, b, a) for a, b in zip(state, other))
        top = jnp.maximum(first[0], second[0])
        scale_a = jnp.exp(first[0] - top)
        scale_b = jnp.exp(second[0] - top)
        total = first[1] * scale_a + second[1] * scale_b
        out = first[2] * scale_a[:, :, None] + second[2] * scale_b[:, :, None]
        state = (top, total, out)
        stride *= 2
    return state


def attend_rows(carry_state, queries, new_keys, new_values, slopes, token_step):
    run_max, run_sum, run_out = carry_state
    head_size = queries.shape[2]
    for earlier in range(len(new_keys)):
        active = earlier <= token_step
        scores = jnp.sum(
            queries.astype(jnp.float32) * new_keys[earlier].astype(jnp.float32), axis=2
        ) * head_size ** (-0.5)
        scores = scores - slopes[None, :] * (token_step - earlier).astype(jnp.float32)
        next_max = jnp.maximum(run_max, scores)
        rescale = jnp.exp(run_max - next_max)
        expon = jnp.exp(scores - next_max)
        weights = lax.optimization_barrier(expon.astype(jnp.bfloat16)).astype(jnp.float32)
        next_sum = run_sum * rescale + expon
        next_out = run_out * rescale[:, :, None] + weights[:, :, None] * new_values[earlier].astype(
            jnp.float32
        )
        run_sum = jnp.where(active, next_sum, run_sum)
        run_out = jnp.where(active, next_out, run_out)
        run_max = jnp.where(active, next_max, run_max)
    attended = (run_out / run_sum[:, :, None]).astype(jnp.bfloat16)
    return attended.reshape(attended.shape[0], -1)


def on_device(
    tokens,
    lengths,
    page_owner,
    page_number,
    key_pages,
    value_pages,
    alibi_slopes,
    norm1_gain,
    norm2_gain,
    w_qkv,
    w_out,
    w_up,
    w_down,
    nseq,
    nhead,
):
    nsteps, requests, local_width = tokens.shape
    nheads = alibi_slopes.shape[0]
    head_width = key_pages.shape[2]
    head_size = head_width // nheads
    nblocks = key_pages.shape[0] // BLK
    qkv_width = w_qkv.shape[1] * w_qkv.shape[2]
    rows = nsteps * requests

    qkv_chunk = qkv_width // nseq
    up_chunk = w_up.shape[1] // nseq
    gain_pair = jnp.stack([norm1_gain, norm2_gain])
    gain_parts = []
    for _ in range(3):
        piece = lax.optimization_barrier(gain_pair.astype(jnp.bfloat16))
        gain_parts.append(piece)
        gain_pair = gain_pair - piece.astype(jnp.float32)

    token_rows = tokens.reshape(rows, local_width)
    token_float = token_rows.astype(jnp.float32)
    gathered = gather_cols(jnp.concatenate([token_rows] + gain_parts, axis=0), nseq)
    qkv_in, gathered = lax.optimization_barrier(
        (w_qkv.reshape(local_width, nseq, qkv_chunk), gathered)
    )
    qkv_cols = lax.all_to_all(qkv_in, "seq", 1, 0, tiled=True).reshape(nseq * local_width, qkv_chunk)
    pieces = gathered[rows:].astype(jnp.float32)
    gains = (pieces[0:2] + pieces[2:4]) + pieces[4:6]
    normed = full_normalize(gathered[:rows], gains[0])
    qkv_part = jnp.dot(normed, qkv_cols, preferred_element_type=jnp.float32).astype(jnp.bfloat16)
    joined = gather_cols(qkv_part, nseq)
    up_in, joined = lax.optimization_barrier((w_up.reshape(local_width, nseq, up_chunk), joined))
    up_cols = lax.all_to_all(up_in, "seq", 1, 0, tiled=True).reshape(nseq * local_width, up_chunk)
    all_queries = joined[:, :head_width].reshape(nsteps, requests, nheads, head_size)
    new_keys = joined[:, head_width : 2 * head_width].reshape(nsteps, requests, nheads, head_size)
    new_values = joined[:, 2 * head_width :].reshape(nsteps, requests, nheads, head_size)

    states = []
    for token_step in range(nsteps):
        queries = all_queries[token_step]
        carry_state = (
            jnp.full((requests, nheads), floor_score, jnp.float32),
            jnp.zeros((requests, nheads), jnp.float32),
            jnp.zeros((requests, nheads, head_size), jnp.float32),
        )

        def visit(turn_index, state_in):
            first_page = (turn_index * BLK).astype(jnp.int32)
            owners = lax.dynamic_slice_in_dim(page_owner, first_page, BLK, 0)
            number = lax.dynamic_slice_in_dim(page_number, first_page, BLK, 0)
            key_block = lax.dynamic_slice_in_dim(key_pages, first_page, BLK, 0)
            value_block = lax.dynamic_slice_in_dim(value_pages, first_page, BLK, 0)

            def compute(state_given):
                return page_block(
                    state_given,
                    owners,
                    number,
                    key_block,
                    value_block,
                    queries,
                    alibi_slopes,
                    lengths,
                    token_step,
                )

            def keep_state(state_given):
                return state_given

            return lax.cond(jnp.any(owners >= 0), compute, keep_state, state_in)

        states.append(lax.fori_loop(0, nblocks, visit, carry_state))

    joined_state = tuple(jnp.concatenate(parts, axis=0) for parts in zip(*states))
    up_cols, (run_max, run_sum, run_out) = lax.optimization_barrier((up_cols, joined_state))
    own_rows = rows // nseq
    stats = jnp.concatenate(
        [
            jnp.swapaxes(run_max.reshape(nseq, own_rows, nheads), 1, 2),
            jnp.swapaxes(run_sum.reshape(nseq, own_rows, nheads), 1, 2),
            jnp.zeros((nseq, nheads, head_size - 2 * own_rows), jnp.float32),
        ],
        axis=2,
    )
    packed = jnp.concatenate(
        [run_out.reshape(nseq, own_rows, nheads, head_size), stats[:, None]], axis=1
    )
    packed = lax.all_to_all(packed, "seq", 0, 0, tiled=True)
    part_out = packed[:, :own_rows]
    part_max = jnp.swapaxes(packed[:, own_rows, :, :own_rows], 1, 2)
    part_sum = jnp.swapaxes(packed[:, own_rows, :, own_rows : 2 * own_rows], 1, 2)
    top_max = jnp.max(part_max, axis=0)
    rescale = jnp.exp(part_max - top_max[None])
    top_sum = jnp.sum(part_sum * rescale, axis=0)
    top_out = jnp.sum(part_out * rescale[:, :, :, None], axis=0)
    first_row = lax.axis_index("seq") * own_rows
    my_step = first_row // requests
    pick = lambda a: lax.dynamic_slice_in_dim(a.reshape(rows, nheads, head_size), first_row, own_rows, 0)
    my_queries = pick(all_queries)
    my_keys = []
    my_values = []
    for earlier in range(nsteps):
        shifted = first_row - (my_step - earlier) * requests
        my_keys.append(lax.dynamic_slice_in_dim(new_keys.reshape(rows, nheads, head_size), shifted, own_rows, 0))
        my_values.append(lax.dynamic_slice_in_dim(new_values.reshape(rows, nheads, head_size), shifted, own_rows, 0))
    mine = attend_rows(
        (top_max, top_sum, top_out), my_queries, my_keys, my_values, alibi_slopes, my_step
    )
    attended = gather_rows(mine, nseq).reshape(rows, -1)
    projected = head_sum(
        lax.dot_general(attended, w_out, (((1,), (1,)), ((), ())), preferred_element_type=jnp.float32),
        nhead,
    )
    hidden_in = (token_float + projected).astype(jnp.bfloat16)
    hidden_float = hidden_in.astype(jnp.float32)
    normed_two = full_normalize(gather_cols(hidden_in, nseq), gains[1])
    up_share = jnp.dot(normed_two, up_cols, preferred_element_type=jnp.float32)
    hidden_share = jax.nn.gelu(up_share, approximate=False).astype(jnp.bfloat16)
    down_part = lax.dot_general(
        gather_cols(hidden_share, nseq),
        w_down,
        (((1,), (1,)), ((), ())),
        preferred_element_type=jnp.float32,
    )
    down_proj = head_sum(down_part, nhead)
    return (hidden_float + down_proj).astype(jnp.bfloat16).reshape(nsteps, requests, local_width)


def solution(mesh):
    placed = (
        P(None, None, "seq"),
        P(),
        P("seq"),
        P("seq"),
        P("seq", None, "head"),
        P("seq", None, "head"),
        P("head"),
        P("seq"),
        P("seq"),
        P("seq", None, "head"),
        P("seq", "head"),
        P("seq", "head"),
        P("seq", "head"),
    )
    nseq = mesh.shape["seq"]
    return jax.shard_map(
        functools.partial(on_device, nseq=nseq, nhead=mesh.shape["head"]), mesh=mesh, in_specs=placed, out_specs=P(None, None, "seq"), check_vma=False
    )
```

```python
import functools

import jax
import jax.numpy as jnp
from jax import lax
from jax.sharding import PartitionSpec as P

D = 4096
BLK = 8


eps_norm = 1e-05
floor_score = -1e30
highest = lax.Precision.HIGHEST


def normalize(token_rows, gain_share, totals, width_all):
    row_sum, row_squares = totals
    mean_value = row_sum / width_all
    variance = row_squares / width_all - mean_value * mean_value
    return (
        (token_rows.astype(jnp.float32) - mean_value[:, None])
        * lax.rsqrt(variance + eps_norm)[:, None]
        * gain_share[None, :]
    ).astype(jnp.bfloat16)


def page_block(carry_state, owners, number, key_block, value_block, queries, slopes, lengths):
    run_max, run_sum, run_out = carry_state
    nblock, page_len, width_all = key_block.shape
    nheads = slopes.shape[0]
    head_size = width_all // nheads
    nsteps, requests = queries.shape[0], queries.shape[1]
    safe_owner = jnp.clip(owners, 0, requests - 1)
    page_query = jnp.take(queries, safe_owner, axis=1)
    key_heads = key_block.reshape(nblock, page_len, nheads, head_size)
    value_heads = value_block.reshape(nblock, page_len, nheads, head_size)
    scores = jnp.einsum(
        "sbhe,bthe->sbth", page_query, key_heads, preferred_element_type=jnp.float32
    ) * head_size ** (-0.5)
    positions = number[:, None] * page_len + jnp.arange(page_len, dtype=jnp.int32)[None, :]
    own_length = jnp.take(lengths, safe_owner)
    step_ids = jnp.arange(nsteps, dtype=jnp.int32)
    distance = (
        own_length[None, :, None] + step_ids[:, None, None] - positions[None]
    ).astype(jnp.float32)
    scores = scores - distance[..., None] * slopes
    valid_mask = (owners[:, None] >= 0) & (positions < own_length[:, None])
    masked = jnp.where(valid_mask[None, :, :, None], scores, floor_score)
    page_max = jnp.max(masked, axis=2)
    member = owners[None, :] == jnp.arange(requests, dtype=jnp.int32)[:, None]
    block_max = jnp.max(
        jnp.where(member[None, :, :, None], page_max[:, None, :, :], floor_score), axis=2
    )
    next_max = jnp.maximum(run_max, block_max)
    owner_max = jnp.take(next_max, safe_owner, axis=1)
    expon = jnp.where(
        valid_mask[None, :, :, None], jnp.exp(masked - owner_max[:, :, None, :]), 0.0
    )
    page_sum = jnp.sum(expon, axis=2)
    weights = expon.astype(jnp.bfloat16)
    page_out = jnp.einsum(
        "sbth,bthe->sbhe", weights, value_heads, preferred_element_type=jnp.float32
    )
    member_float = member.astype(jnp.float32)
    rescale = jnp.exp(run_max - next_max)
    next_sum = run_sum * rescale + jnp.einsum(
        "rb,sbh->srh", member_float, page_sum, precision=highest
    )
    added = jnp.einsum(
        "rb,sbx->srx", member_float, page_out.reshape(nsteps, nblock, nheads * head_size),
        precision=highest,
    )
    next_out = run_out * rescale[..., None] + added.reshape(nsteps, requests, nheads, head_size)
    return (next_max, next_sum, next_out)


def attend_new(carry_state, queries, new_keys, new_values, slopes, token_step):
    run_max, run_sum, run_out = carry_state
    head_size = queries.shape[2]
    for earlier in range(token_step + 1):
        scores = jnp.sum(
            queries.astype(jnp.float32) * new_keys[earlier].astype(jnp.float32), axis=2
        ) * head_size ** (-0.5)
        scores = scores - slopes[None, :] * float(token_step - earlier)
        next_max = jnp.maximum(run_max, scores)
        rescale = jnp.exp(run_max - next_max)
        expon = jnp.exp(scores - next_max)
        weights = lax.optimization_barrier(expon.astype(jnp.bfloat16)).astype(jnp.float32)
        run_sum = run_sum * rescale + expon
        run_out = run_out * rescale[:, :, None] + weights[:, :, None] * new_values[earlier].astype(
            jnp.float32
        )
        run_max = next_max
    attended = (run_out / run_sum[:, :, None]).astype(jnp.bfloat16)
    return attended.reshape(attended.shape[0], -1)


def gather_rows(part, nseq):
    copies = jnp.broadcast_to(part[None], (nseq,) + part.shape)
    return lax.all_to_all(copies, "seq", 0, 0, tiled=True)


def gather_cols(part, nseq):
    got = gather_rows(part, nseq)
    return jnp.moveaxis(got, 0, -2).reshape(part.shape[:-1] + (nseq * part.shape[-1],))


def head_sum(part, nhead):
    my_index = lax.axis_index("head")
    stride = 1
    while stride < nhead:
        other = lax.ppermute(part, "head", [(i, i ^ stride) for i in range(nhead)])
        low = (my_index & stride) == 0
        part = jnp.where(low, part + other, other + part)
        stride *= 2
    return part


def full_normalize(rows, gain_full):
    row_float = rows.astype(jnp.float32)
    totals = (jnp.sum(row_float, axis=1), jnp.sum(row_float * row_float, axis=1))
    return normalize(rows, gain_full, totals, rows.shape[1])


def butterfly_combine(state, nseq):
    my_index = lax.axis_index("seq")
    stride = 1
    while stride < nseq:
        pairs = [(i, i ^ stride) for i in range(nseq)]
        other = lax.ppermute(state, "seq", pairs)
        low = (my_index & stride) == 0
        first = tuple(jnp.where(low, a, b) for a, b in zip(state, other))
        second = tuple(jnp.where(low, b, a) for a, b in zip(state, other))
        top = jnp.maximum(first[0], second[0])
        scale_a = jnp.exp(first[0] - top)
        scale_b = jnp.exp(second[0] - top)
        total = first[1] * scale_a + second[1] * scale_b
        out = first[2] * scale_a[:, :, None] + second[2] * scale_b[:, :, None]
        state = (top, total, out)
        stride *= 2
    return state


def attend_rows(carry_state, queries, new_keys, new_values, slopes, token_step):
    run_max, run_sum, run_out = carry_state
    head_size = queries.shape[2]
    for earlier in range(len(new_keys)):
        active = earlier <= token_step
        scores = jnp.sum(
            queries.astype(jnp.float32) * new_keys[earlier].astype(jnp.float32), axis=2
        ) * head_size ** (-0.5)
        scores = scores - slopes[None, :] * (token_step - earlier).astype(jnp.float32)
        next_max = jnp.maximum(run_max, scores)
        rescale = jnp.exp(run_max - next_max)
        expon = jnp.exp(scores - next_max)
        weights = lax.optimization_barrier(expon.astype(jnp.bfloat16)).astype(jnp.float32)
        next_sum = run_sum * rescale + expon
        next_out = run_out * rescale[:, :, None] + weights[:, :, None] * new_values[earlier].astype(
            jnp.float32
        )
        run_sum = jnp.where(active, next_sum, run_sum)
        run_out = jnp.where(active, next_out, run_out)
        run_max = jnp.where(active, next_max, run_max)
    attended = (run_out / run_sum[:, :, None]).astype(jnp.bfloat16)
    return attended.reshape(attended.shape[0], -1)


def on_device(
    tokens,
    lengths,
    page_owner,
    page_number,
    key_pages,
    value_pages,
    alibi_slopes,
    norm1_gain,
    norm2_gain,
    w_qkv,
    w_out,
    w_up,
    w_down,
    nseq,
    nhead,
):
    nsteps, requests, local_width = tokens.shape
    nheads = alibi_slopes.shape[0]
    head_width = key_pages.shape[2]
    head_size = head_width // nheads
    nblocks = key_pages.shape[0] // BLK
    qkv_width = w_qkv.shape[1] * w_qkv.shape[2]
    rows = nsteps * requests

    qkv_chunk = qkv_width // nseq
    up_chunk = w_up.shape[1] // nseq
    gain_pair = jnp.stack([norm1_gain, norm2_gain])
    gain_parts = []
    for _ in range(3):
        piece = lax.optimization_barrier(gain_pair.astype(jnp.bfloat16))
        gain_parts.append(piece)
        gain_pair = gain_pair - piece.astype(jnp.float32)

    token_rows = tokens.reshape(rows, local_width)
    token_float = token_rows.astype(jnp.float32)
    gathered = gather_cols(jnp.concatenate([token_rows] + gain_parts, axis=0), nseq)
    qkv_in, gathered = lax.optimization_barrier(
        (w_qkv.reshape(local_width, nseq, qkv_chunk), gathered)
    )
    qkv_cols = lax.all_to_all(qkv_in, "seq", 1, 0, tiled=True).reshape(nseq * local_width, qkv_chunk)
    pieces = gathered[rows:].astype(jnp.float32)
    gains = (pieces[0:2] + pieces[2:4]) + pieces[4:6]
    normed = full_normalize(gathered[:rows], gains[0])
    qkv_part = jnp.dot(normed, qkv_cols, preferred_element_type=jnp.float32).astype(jnp.bfloat16)
    joined = gather_cols(qkv_part, nseq)
    up_in, joined = lax.optimization_barrier((w_up.reshape(local_width, nseq, up_chunk), joined))
    up_cols = lax.all_to_all(up_in, "seq", 1, 0, tiled=True).reshape(nseq * local_width, up_chunk)
    all_queries = joined[:, :head_width].reshape(nsteps, requests, nheads, head_size)
    new_keys = joined[:, head_width : 2 * head_width].reshape(nsteps, requests, nheads, head_size)
    new_values = joined[:, 2 * head_width :].reshape(nsteps, requests, nheads, head_size)

    carry_state = (
        jnp.full((nsteps, requests, nheads), floor_score, jnp.float32),
        jnp.zeros((nsteps, requests, nheads), jnp.float32),
        jnp.zeros((nsteps, requests, nheads, head_size), jnp.float32),
    )

    def visit(turn_index, state_in):
        first_page = (turn_index * BLK).astype(jnp.int32)
        owners = lax.dynamic_slice_in_dim(page_owner, first_page, BLK, 0)
        number = lax.dynamic_slice_in_dim(page_number, first_page, BLK, 0)
        key_block = lax.dynamic_slice_in_dim(key_pages, first_page, BLK, 0)
        value_block = lax.dynamic_slice_in_dim(value_pages, first_page, BLK, 0)

        def compute(state_given):
            return page_block(
                state_given, owners, number, key_block, value_block, all_queries, alibi_slopes, lengths
            )

        def keep_state(state_given):
            return state_given

        return lax.cond(jnp.any(owners >= 0), compute, keep_state, state_in)

    final_state = lax.fori_loop(0, nblocks, visit, carry_state)

    joined_state = tuple(part.reshape((rows,) + part.shape[2:]) for part in final_state)
    up_cols, (run_max, run_sum, run_out) = lax.optimization_barrier((up_cols, joined_state))
    own_rows = rows // nseq
    stats = jnp.concatenate(
        [
            jnp.swapaxes(run_max.reshape(nseq, own_rows, nheads), 1, 2),
            jnp.swapaxes(run_sum.reshape(nseq, own_rows, nheads), 1, 2),
            jnp.zeros((nseq, nheads, head_size - 2 * own_rows), jnp.float32),
        ],
        axis=2,
    )
    packed = jnp.concatenate(
        [run_out.reshape(nseq, own_rows, nheads, head_size), stats[:, None]], axis=1
    )
    packed = lax.all_to_all(packed, "seq", 0, 0, tiled=True)
    part_out = packed[:, :own_rows]
    part_max = jnp.swapaxes(packed[:, own_rows, :, :own_rows], 1, 2)
    part_sum = jnp.swapaxes(packed[:, own_rows, :, own_rows : 2 * own_rows], 1, 2)
    top_max = jnp.max(part_max, axis=0)
    rescale = jnp.exp(part_max - top_max[None])
    top_sum = jnp.sum(part_sum * rescale, axis=0)
    top_out = jnp.sum(part_out * rescale[:, :, :, None], axis=0)
    first_row = lax.axis_index("seq") * own_rows
    my_step = first_row // requests
    pick = lambda a: lax.dynamic_slice_in_dim(a.reshape(rows, nheads, head_size), first_row, own_rows, 0)
    my_queries = pick(all_queries)
    my_keys = []
    my_values = []
    for earlier in range(nsteps):
        shifted = first_row - (my_step - earlier) * requests
        my_keys.append(lax.dynamic_slice_in_dim(new_keys.reshape(rows, nheads, head_size), shifted, own_rows, 0))
        my_values.append(lax.dynamic_slice_in_dim(new_values.reshape(rows, nheads, head_size), shifted, own_rows, 0))
    mine = attend_rows(
        (top_max, top_sum, top_out), my_queries, my_keys, my_values, alibi_slopes, my_step
    )
    attended = gather_rows(mine, nseq).reshape(rows, -1)
    projected = head_sum(
        lax.dot_general(attended, w_out, (((1,), (1,)), ((), ())), preferred_element_type=jnp.float32),
        nhead,
    )
    hidden_in = (token_float + projected).astype(jnp.bfloat16)
    hidden_float = hidden_in.astype(jnp.float32)
    normed_two = full_normalize(gather_cols(hidden_in, nseq), gains[1])
    up_share = jnp.dot(normed_two, up_cols, preferred_element_type=jnp.float32)
    hidden_share = jax.nn.gelu(up_share, approximate=False).astype(jnp.bfloat16)
    down_part = lax.dot_general(
        gather_cols(hidden_share, nseq),
        w_down,
        (((1,), (1,)), ((), ())),
        preferred_element_type=jnp.float32,
    )
    down_proj = head_sum(down_part, nhead)
    return (hidden_float + down_proj).astype(jnp.bfloat16).reshape(nsteps, requests, local_width)


def solution(mesh):
    placed = (
        P(None, None, "seq"),
        P(),
        P("seq"),
        P("seq"),
        P("seq", None, "head"),
        P("seq", None, "head"),
        P("head"),
        P("seq"),
        P("seq"),
        P("seq", None, "head"),
        P("seq", "head"),
        P("seq", "head"),
        P("seq", "head"),
    )
    nseq = mesh.shape["seq"]
    return jax.shard_map(
        functools.partial(on_device, nseq=nseq, nhead=mesh.shape["head"]), mesh=mesh, in_specs=placed, out_specs=P(None, None, "seq"), check_vma=False
    )
```

```python
import functools

import jax
import jax.numpy as jnp
from jax import lax
from jax.sharding import PartitionSpec as P

D = 4096
BLK = 8


eps_norm = 1e-05
floor_score = -1e30
highest = lax.Precision.HIGHEST


def normalize(token_rows, gain_share, totals, width_all):
    row_sum, row_squares = totals
    mean_value = row_sum / width_all
    variance = row_squares / width_all - mean_value * mean_value
    return (
        (token_rows.astype(jnp.float32) - mean_value[:, None])
        * lax.rsqrt(variance + eps_norm)[:, None]
        * gain_share[None, :]
    ).astype(jnp.bfloat16)


def page_block(carry_state, owners, number, key_block, value_block, queries, slopes, lengths):
    run_max, run_sum, run_out = carry_state
    nblock, page_len, width_all = key_block.shape
    nheads = slopes.shape[0]
    head_size = width_all // nheads
    nsteps, requests = queries.shape[0], queries.shape[1]
    safe_owner = jnp.clip(owners, 0, requests - 1)
    page_query = jnp.take(queries, safe_owner, axis=1)
    key_heads = key_block.reshape(nblock, page_len, nheads, head_size)
    value_heads = value_block.reshape(nblock, page_len, nheads, head_size)
    scores = jnp.einsum(
        "sbhe,bthe->sbth", page_query, key_heads, preferred_element_type=jnp.float32
    ) * head_size ** (-0.5)
    positions = number[:, None] * page_len + jnp.arange(page_len, dtype=jnp.int32)[None, :]
    own_length = jnp.take(lengths, safe_owner)
    step_ids = jnp.arange(nsteps, dtype=jnp.int32)
    distance = (
        own_length[None, :, None] + step_ids[:, None, None] - positions[None]
    ).astype(jnp.float32)
    scores = scores - distance[..., None] * slopes
    valid_mask = (owners[:, None] >= 0) & (positions < own_length[:, None])
    masked = jnp.where(valid_mask[None, :, :, None], scores, floor_score)
    page_max = jnp.max(masked, axis=2)
    member = owners[None, :] == jnp.arange(requests, dtype=jnp.int32)[:, None]
    block_max = jnp.max(
        jnp.where(member[None, :, :, None], page_max[:, None, :, :], floor_score), axis=2
    )
    next_max = jnp.maximum(run_max, block_max)
    owner_max = jnp.take(next_max, safe_owner, axis=1)
    expon = jnp.where(
        valid_mask[None, :, :, None], jnp.exp(masked - owner_max[:, :, None, :]), 0.0
    )
    page_sum = jnp.sum(expon, axis=2)
    weights = expon.astype(jnp.bfloat16)
    page_out = jnp.einsum(
        "sbth,bthe->sbhe", weights, value_heads, preferred_element_type=jnp.float32
    )
    member_float = member.astype(jnp.float32)
    rescale = jnp.exp(run_max - next_max)
    next_sum = run_sum * rescale + jnp.einsum(
        "rb,sbh->srh", member_float, page_sum, precision=highest
    )
    added = jnp.einsum(
        "rb,sbx->srx", member_float, page_out.reshape(nsteps, nblock, nheads * head_size),
        precision=highest,
    )
    next_out = run_out * rescale[..., None] + added.reshape(nsteps, requests, nheads, head_size)
    return (next_max, next_sum, next_out)


def attend_new(carry_state, queries, new_keys, new_values, slopes, token_step):
    run_max, run_sum, run_out = carry_state
    head_size = queries.shape[2]
    for earlier in range(token_step + 1):
        scores = jnp.sum(
            queries.astype(jnp.float32) * new_keys[earlier].astype(jnp.float32), axis=2
        ) * head_size ** (-0.5)
        scores = scores - slopes[None, :] * float(token_step - earlier)
        next_max = jnp.maximum(run_max, scores)
        rescale = jnp.exp(run_max - next_max)
        expon = jnp.exp(scores - next_max)
        weights = lax.optimization_barrier(expon.astype(jnp.bfloat16)).astype(jnp.float32)
        run_sum = run_sum * rescale + expon
        run_out = run_out * rescale[:, :, None] + weights[:, :, None] * new_values[earlier].astype(
            jnp.float32
        )
        run_max = next_max
    attended = (run_out / run_sum[:, :, None]).astype(jnp.bfloat16)
    return attended.reshape(attended.shape[0], -1)


def gather_rows(part, nseq):
    copies = jnp.broadcast_to(part[None], (nseq,) + part.shape)
    return lax.all_to_all(copies, "seq", 0, 0, tiled=True)


def gather_cols(part, nseq):
    got = gather_rows(part, nseq)
    return jnp.moveaxis(got, 0, -2).reshape(part.shape[:-1] + (nseq * part.shape[-1],))


def head_sum(part, nhead):
    my_index = lax.axis_index("head")
    stride = 1
    while stride < nhead:
        other = lax.ppermute(part, "head", [(i, i ^ stride) for i in range(nhead)])
        low = (my_index & stride) == 0
        part = jnp.where(low, part + other, other + part)
        stride *= 2
    return part


def full_normalize(rows, gain_full):
    row_float = rows.astype(jnp.float32)
    totals = (jnp.sum(row_float, axis=1), jnp.sum(row_float * row_float, axis=1))
    return normalize(rows, gain_full, totals, rows.shape[1])


def butterfly_combine(state, nseq):
    my_index = lax.axis_index("seq")
    stride = 1
    while stride < nseq:
        pairs = [(i, i ^ stride) for i in range(nseq)]
        other = lax.ppermute(state, "seq", pairs)
        low = (my_index & stride) == 0
        first = tuple(jnp.where(low, a, b) for a, b in zip(state, other))
        second = tuple(jnp.where(low, b, a) for a, b in zip(state, other))
        top = jnp.maximum(first[0], second[0])
        scale_a = jnp.exp(first[0] - top)
        scale_b = jnp.exp(second[0] - top)
        total = first[1] * scale_a + second[1] * scale_b
        out = first[2] * scale_a[:, :, None] + second[2] * scale_b[:, :, None]
        state = (top, total, out)
        stride *= 2
    return state


def attend_rows(carry_state, queries, new_keys, new_values, slopes, token_step):
    run_max, run_sum, run_out = carry_state
    head_size = queries.shape[2]
    for earlier in range(len(new_keys)):
        active = earlier <= token_step
        scores = jnp.sum(
            queries.astype(jnp.float32) * new_keys[earlier].astype(jnp.float32), axis=2
        ) * head_size ** (-0.5)
        scores = scores - slopes[None, :] * (token_step - earlier).astype(jnp.float32)
        next_max = jnp.maximum(run_max, scores)
        rescale = jnp.exp(run_max - next_max)
        expon = jnp.exp(scores - next_max)
        weights = lax.optimization_barrier(expon.astype(jnp.bfloat16)).astype(jnp.float32)
        next_sum = run_sum * rescale + expon
        next_out = run_out * rescale[:, :, None] + weights[:, :, None] * new_values[earlier].astype(
            jnp.float32
        )
        run_sum = jnp.where(active, next_sum, run_sum)
        run_out = jnp.where(active, next_out, run_out)
        run_max = jnp.where(active, next_max, run_max)
    attended = (run_out / run_sum[:, :, None]).astype(jnp.bfloat16)
    return attended.reshape(attended.shape[0], -1)


def on_device(
    tokens,
    lengths,
    page_owner,
    page_number,
    key_pages,
    value_pages,
    alibi_slopes,
    norm1_gain,
    norm2_gain,
    w_qkv,
    w_out,
    w_up,
    w_down,
    nseq,
    nhead,
):
    nsteps, requests, local_width = tokens.shape
    nheads = alibi_slopes.shape[0]
    head_width = key_pages.shape[2]
    head_size = head_width // nheads
    qkv_width = w_qkv.shape[1] * w_qkv.shape[2]
    rows = nsteps * requests

    qkv_chunk = qkv_width // nseq
    up_chunk = w_up.shape[1] // nseq
    gain_pair = jnp.stack([norm1_gain, norm2_gain])
    gain_parts = []
    for _ in range(3):
        piece = lax.optimization_barrier(gain_pair.astype(jnp.bfloat16))
        gain_parts.append(piece)
        gain_pair = gain_pair - piece.astype(jnp.float32)

    token_rows = tokens.reshape(rows, local_width)
    token_float = token_rows.astype(jnp.float32)
    gathered = gather_cols(jnp.concatenate([token_rows] + gain_parts, axis=0), nseq)
    qkv_in, gathered = lax.optimization_barrier(
        (w_qkv.reshape(local_width, nseq, qkv_chunk), gathered)
    )
    qkv_cols = lax.all_to_all(qkv_in, "seq", 1, 0, tiled=True).reshape(nseq * local_width, qkv_chunk)
    pieces = gathered[rows:].astype(jnp.float32)
    gains = (pieces[0:2] + pieces[2:4]) + pieces[4:6]
    normed = full_normalize(gathered[:rows], gains[0])
    qkv_part = jnp.dot(normed, qkv_cols, preferred_element_type=jnp.float32).astype(jnp.bfloat16)
    joined = gather_cols(qkv_part, nseq)
    up_in, joined = lax.optimization_barrier((w_up.reshape(local_width, nseq, up_chunk), joined))
    up_cols = lax.all_to_all(up_in, "seq", 1, 0, tiled=True).reshape(nseq * local_width, up_chunk)
    all_queries = joined[:, :head_width].reshape(nsteps, requests, nheads, head_size)
    new_keys = joined[:, head_width : 2 * head_width].reshape(nsteps, requests, nheads, head_size)
    new_values = joined[:, 2 * head_width :].reshape(nsteps, requests, nheads, head_size)

    carry_state = (
        jnp.full((nsteps, requests, nheads), floor_score, jnp.float32),
        jnp.zeros((nsteps, requests, nheads), jnp.float32),
        jnp.zeros((nsteps, requests, nheads, head_size), jnp.float32),
    )

    final_state = page_block(
        carry_state, page_owner, page_number, key_pages, value_pages, all_queries, alibi_slopes, lengths
    )

    joined_state = tuple(part.reshape((rows,) + part.shape[2:]) for part in final_state)
    up_cols, (run_max, run_sum, run_out) = lax.optimization_barrier((up_cols, joined_state))
    own_rows = rows // nseq
    stats = jnp.concatenate(
        [
            jnp.swapaxes(run_max.reshape(nseq, own_rows, nheads), 1, 2),
            jnp.swapaxes(run_sum.reshape(nseq, own_rows, nheads), 1, 2),
            jnp.zeros((nseq, nheads, head_size - 2 * own_rows), jnp.float32),
        ],
        axis=2,
    )
    packed = jnp.concatenate(
        [run_out.reshape(nseq, own_rows, nheads, head_size), stats[:, None]], axis=1
    )
    packed = lax.all_to_all(packed, "seq", 0, 0, tiled=True)
    part_out = packed[:, :own_rows]
    part_max = jnp.swapaxes(packed[:, own_rows, :, :own_rows], 1, 2)
    part_sum = jnp.swapaxes(packed[:, own_rows, :, own_rows : 2 * own_rows], 1, 2)
    top_max = jnp.max(part_max, axis=0)
    rescale = jnp.exp(part_max - top_max[None])
    top_sum = jnp.sum(part_sum * rescale, axis=0)
    top_out = jnp.sum(part_out * rescale[:, :, :, None], axis=0)
    first_row = lax.axis_index("seq") * own_rows
    my_step = first_row // requests
    pick = lambda a: lax.dynamic_slice_in_dim(a.reshape(rows, nheads, head_size), first_row, own_rows, 0)
    my_queries = pick(all_queries)
    my_keys = []
    my_values = []
    for earlier in range(nsteps):
        shifted = first_row - (my_step - earlier) * requests
        my_keys.append(lax.dynamic_slice_in_dim(new_keys.reshape(rows, nheads, head_size), shifted, own_rows, 0))
        my_values.append(lax.dynamic_slice_in_dim(new_values.reshape(rows, nheads, head_size), shifted, own_rows, 0))
    mine = attend_rows(
        (top_max, top_sum, top_out), my_queries, my_keys, my_values, alibi_slopes, my_step
    )
    attended = gather_rows(mine, nseq).reshape(rows, -1)
    projected = head_sum(
        lax.dot_general(attended, w_out, (((1,), (1,)), ((), ())), preferred_element_type=jnp.float32),
        nhead,
    )
    hidden_in = (token_float + projected).astype(jnp.bfloat16)
    hidden_float = hidden_in.astype(jnp.float32)
    normed_two = full_normalize(gather_cols(hidden_in, nseq), gains[1])
    up_share = jnp.dot(normed_two, up_cols, preferred_element_type=jnp.float32)
    hidden_share = jax.nn.gelu(up_share, approximate=False).astype(jnp.bfloat16)
    down_part = lax.dot_general(
        gather_cols(hidden_share, nseq),
        w_down,
        (((1,), (1,)), ((), ())),
        preferred_element_type=jnp.float32,
    )
    down_proj = head_sum(down_part, nhead)
    return (hidden_float + down_proj).astype(jnp.bfloat16).reshape(nsteps, requests, local_width)


def solution(mesh):
    placed = (
        P(None, None, "seq"),
        P(),
        P("seq"),
        P("seq"),
        P("seq", None, "head"),
        P("seq", None, "head"),
        P("head"),
        P("seq"),
        P("seq"),
        P("seq", None, "head"),
        P("seq", "head"),
        P("seq", "head"),
        P("seq", "head"),
    )
    nseq = mesh.shape["seq"]
    return jax.shard_map(
        functools.partial(on_device, nseq=nseq, nhead=mesh.shape["head"]), mesh=mesh, in_specs=placed, out_specs=P(None, None, "seq"), check_vma=False
    )
```

```python
import functools

import jax
import jax.numpy as jnp
from jax import lax
from jax.sharding import PartitionSpec as P

D = 4096
BLK = 8


eps_norm = 1e-05
floor_score = -1e30
highest = lax.Precision.HIGHEST


def normalize(token_rows, gain_share, totals, width_all):
    row_sum, row_squares = totals
    mean_value = row_sum / width_all
    variance = row_squares / width_all - mean_value * mean_value
    return (
        (token_rows.astype(jnp.float32) - mean_value[:, None])
        * lax.rsqrt(variance + eps_norm)[:, None]
        * gain_share[None, :]
    ).astype(jnp.bfloat16)


def page_block(carry_state, owners, number, key_block, value_block, queries, slopes, lengths):
    run_max, run_sum, run_out = carry_state
    nblock, page_len, width_all = key_block.shape
    nheads = slopes.shape[0]
    head_size = width_all // nheads
    nsteps, requests = queries.shape[0], queries.shape[1]
    safe_owner = jnp.clip(owners, 0, requests - 1)
    page_query = jnp.take(queries, safe_owner, axis=1)
    key_heads = key_block.reshape(nblock, page_len, nheads, head_size)
    value_heads = value_block.reshape(nblock, page_len, nheads, head_size)
    scores = jnp.einsum(
        "sbhe,bthe->sbth", page_query, key_heads, preferred_element_type=jnp.float32
    ) * head_size ** (-0.5)
    positions = number[:, None] * page_len + jnp.arange(page_len, dtype=jnp.int32)[None, :]
    own_length = jnp.take(lengths, safe_owner)
    step_ids = jnp.arange(nsteps, dtype=jnp.int32)
    distance = (
        own_length[None, :, None] + step_ids[:, None, None] - positions[None]
    ).astype(jnp.float32)
    scores = scores - distance[..., None] * slopes
    valid_mask = (owners[:, None] >= 0) & (positions < own_length[:, None])
    masked = jnp.where(valid_mask[None, :, :, None], scores, floor_score)
    page_max = jnp.max(masked, axis=2)
    member = owners[None, :] == jnp.arange(requests, dtype=jnp.int32)[:, None]
    block_max = jnp.max(
        jnp.where(member[None, :, :, None], page_max[:, None, :, :], floor_score), axis=2
    )
    next_max = jnp.maximum(run_max, block_max)
    owner_max = jnp.take(next_max, safe_owner, axis=1)
    expon = jnp.where(
        valid_mask[None, :, :, None], jnp.exp(masked - owner_max[:, :, None, :]), 0.0
    )
    page_sum = jnp.sum(expon, axis=2)
    weights = expon.astype(jnp.bfloat16)
    page_out = jnp.einsum(
        "sbth,bthe->sbhe", weights, value_heads, preferred_element_type=jnp.float32
    )
    member_float = member.astype(jnp.float32)
    rescale = jnp.exp(run_max - next_max)
    next_sum = run_sum * rescale + jnp.einsum(
        "rb,sbh->srh", member_float, page_sum, precision=highest
    )
    added = jnp.einsum(
        "rb,sbx->srx", member_float, page_out.reshape(nsteps, nblock, nheads * head_size),
        precision=highest,
    )
    next_out = run_out * rescale[..., None] + added.reshape(nsteps, requests, nheads, head_size)
    return (next_max, next_sum, next_out)


def attend_new(carry_state, queries, new_keys, new_values, slopes, token_step):
    run_max, run_sum, run_out = carry_state
    head_size = queries.shape[2]
    for earlier in range(token_step + 1):
        scores = jnp.sum(
            queries.astype(jnp.float32) * new_keys[earlier].astype(jnp.float32), axis=2
        ) * head_size ** (-0.5)
        scores = scores - slopes[None, :] * float(token_step - earlier)
        next_max = jnp.maximum(run_max, scores)
        rescale = jnp.exp(run_max - next_max)
        expon = jnp.exp(scores - next_max)
        weights = lax.optimization_barrier(expon.astype(jnp.bfloat16)).astype(jnp.float32)
        run_sum = run_sum * rescale + expon
        run_out = run_out * rescale[:, :, None] + weights[:, :, None] * new_values[earlier].astype(
            jnp.float32
        )
        run_max = next_max
    attended = (run_out / run_sum[:, :, None]).astype(jnp.bfloat16)
    return attended.reshape(attended.shape[0], -1)


def gather_rows(part, nseq):
    copies = jnp.broadcast_to(part[None], (nseq,) + part.shape)
    return lax.all_to_all(copies, "seq", 0, 0, tiled=True)


def gather_cols(part, nseq):
    got = gather_rows(part, nseq)
    return jnp.moveaxis(got, 0, -2).reshape(part.shape[:-1] + (nseq * part.shape[-1],))


def head_sum(part, nhead):
    my_index = lax.axis_index("head")
    stride = 1
    while stride < nhead:
        other = lax.ppermute(part, "head", [(i, i ^ stride) for i in range(nhead)])
        low = (my_index & stride) == 0
        part = jnp.where(low, part + other, other + part)
        stride *= 2
    return part


def full_normalize(rows, gain_full):
    row_float = rows.astype(jnp.float32)
    totals = (jnp.sum(row_float, axis=1), jnp.sum(row_float * row_float, axis=1))
    return normalize(rows, gain_full, totals, rows.shape[1])


def butterfly_combine(state, nseq):
    my_index = lax.axis_index("seq")
    stride = 1
    while stride < nseq:
        pairs = [(i, i ^ stride) for i in range(nseq)]
        other = lax.ppermute(state, "seq", pairs)
        low = (my_index & stride) == 0
        first = tuple(jnp.where(low, a, b) for a, b in zip(state, other))
        second = tuple(jnp.where(low, b, a) for a, b in zip(state, other))
        top = jnp.maximum(first[0], second[0])
        scale_a = jnp.exp(first[0] - top)
        scale_b = jnp.exp(second[0] - top)
        total = first[1] * scale_a + second[1] * scale_b
        out = first[2] * scale_a[:, :, None] + second[2] * scale_b[:, :, None]
        state = (top, total, out)
        stride *= 2
    return state


def attend_rows(carry_state, queries, new_keys, new_values, slopes, token_step):
    run_max, run_sum, run_out = carry_state
    head_size = queries.shape[2]
    for earlier in range(len(new_keys)):
        active = earlier <= token_step
        scores = jnp.sum(
            queries.astype(jnp.float32) * new_keys[earlier].astype(jnp.float32), axis=2
        ) * head_size ** (-0.5)
        scores = scores - slopes[None, :] * (token_step - earlier).astype(jnp.float32)
        next_max = jnp.maximum(run_max, scores)
        rescale = jnp.exp(run_max - next_max)
        expon = jnp.exp(scores - next_max)
        weights = lax.optimization_barrier(expon.astype(jnp.bfloat16)).astype(jnp.float32)
        next_sum = run_sum * rescale + expon
        next_out = run_out * rescale[:, :, None] + weights[:, :, None] * new_values[earlier].astype(
            jnp.float32
        )
        run_sum = jnp.where(active, next_sum, run_sum)
        run_out = jnp.where(active, next_out, run_out)
        run_max = jnp.where(active, next_max, run_max)
    attended = (run_out / run_sum[:, :, None]).astype(jnp.bfloat16)
    return attended.reshape(attended.shape[0], -1)


def on_device(
    tokens,
    lengths,
    page_owner,
    page_number,
    key_pages,
    value_pages,
    alibi_slopes,
    norm1_gain,
    norm2_gain,
    w_qkv,
    w_out,
    w_up,
    w_down,
    nseq,
    nhead,
):
    nsteps, requests, local_width = tokens.shape
    nheads = alibi_slopes.shape[0]
    head_width = key_pages.shape[2]
    head_size = head_width // nheads
    qkv_width = w_qkv.shape[1] * w_qkv.shape[2]
    rows = nsteps * requests

    qkv_chunk = qkv_width // nseq
    up_chunk = w_up.shape[1] // nseq
    gain_pair = jnp.stack([norm1_gain, norm2_gain])
    gain_parts = []
    for _ in range(3):
        piece = lax.optimization_barrier(gain_pair.astype(jnp.bfloat16))
        gain_parts.append(piece)
        gain_pair = gain_pair - piece.astype(jnp.float32)

    both = jnp.concatenate(
        [
            w_qkv.reshape(local_width, nseq, qkv_chunk),
            w_up.reshape(local_width, nseq, up_chunk),
        ],
        axis=2,
    )
    both = lax.all_to_all(both, "seq", 1, 0, tiled=True).reshape(nseq * local_width, qkv_chunk + up_chunk)
    qkv_cols = both[:, :qkv_chunk]
    up_cols = both[:, qkv_chunk:]
    token_rows = tokens.reshape(rows, local_width)
    token_float = token_rows.astype(jnp.float32)
    gathered = gather_cols(jnp.concatenate([token_rows] + gain_parts, axis=0), nseq)
    pieces = gathered[rows:].astype(jnp.float32)
    gains = (pieces[0:2] + pieces[2:4]) + pieces[4:6]
    normed = full_normalize(gathered[:rows], gains[0])
    qkv_part = jnp.dot(normed, qkv_cols, preferred_element_type=jnp.float32).astype(jnp.bfloat16)
    joined = gather_cols(qkv_part, nseq)
    all_queries = joined[:, :head_width].reshape(nsteps, requests, nheads, head_size)
    new_keys = joined[:, head_width : 2 * head_width].reshape(nsteps, requests, nheads, head_size)
    new_values = joined[:, 2 * head_width :].reshape(nsteps, requests, nheads, head_size)

    carry_state = (
        jnp.full((nsteps, requests, nheads), floor_score, jnp.float32),
        jnp.zeros((nsteps, requests, nheads), jnp.float32),
        jnp.zeros((nsteps, requests, nheads, head_size), jnp.float32),
    )

    final_state = page_block(
        carry_state, page_owner, page_number, key_pages, value_pages, all_queries, alibi_slopes, lengths
    )

    joined_state = tuple(part.reshape((rows,) + part.shape[2:]) for part in final_state)
    run_max, run_sum, run_out = joined_state
    own_rows = rows // nseq
    stats = jnp.concatenate(
        [
            jnp.swapaxes(run_max.reshape(nseq, own_rows, nheads), 1, 2),
            jnp.swapaxes(run_sum.reshape(nseq, own_rows, nheads), 1, 2),
            jnp.zeros((nseq, nheads, head_size - 2 * own_rows), jnp.float32),
        ],
        axis=2,
    )
    packed = jnp.concatenate(
        [run_out.reshape(nseq, own_rows, nheads, head_size), stats[:, None]], axis=1
    )
    packed = lax.all_to_all(packed, "seq", 0, 0, tiled=True)
    part_out = packed[:, :own_rows]
    part_max = jnp.swapaxes(packed[:, own_rows, :, :own_rows], 1, 2)
    part_sum = jnp.swapaxes(packed[:, own_rows, :, own_rows : 2 * own_rows], 1, 2)
    top_max = jnp.max(part_max, axis=0)
    rescale = jnp.exp(part_max - top_max[None])
    top_sum = jnp.sum(part_sum * rescale, axis=0)
    top_out = jnp.sum(part_out * rescale[:, :, :, None], axis=0)
    first_row = lax.axis_index("seq") * own_rows
    my_step = first_row // requests
    pick = lambda a: lax.dynamic_slice_in_dim(a.reshape(rows, nheads, head_size), first_row, own_rows, 0)
    my_queries = pick(all_queries)
    my_keys = []
    my_values = []
    for earlier in range(nsteps):
        shifted = first_row - (my_step - earlier) * requests
        my_keys.append(lax.dynamic_slice_in_dim(new_keys.reshape(rows, nheads, head_size), shifted, own_rows, 0))
        my_values.append(lax.dynamic_slice_in_dim(new_values.reshape(rows, nheads, head_size), shifted, own_rows, 0))
    mine = attend_rows(
        (top_max, top_sum, top_out), my_queries, my_keys, my_values, alibi_slopes, my_step
    )
    attended = gather_rows(mine, nseq).reshape(rows, -1)
    projected = head_sum(
        lax.dot_general(attended, w_out, (((1,), (1,)), ((), ())), preferred_element_type=jnp.float32),
        nhead,
    )
    hidden_in = (token_float + projected).astype(jnp.bfloat16)
    hidden_float = hidden_in.astype(jnp.float32)
    normed_two = full_normalize(gather_cols(hidden_in, nseq), gains[1])
    up_share = jnp.dot(normed_two, up_cols, preferred_element_type=jnp.float32)
    hidden_share = jax.nn.gelu(up_share, approximate=False).astype(jnp.bfloat16)
    down_part = lax.dot_general(
        gather_cols(hidden_share, nseq),
        w_down,
        (((1,), (1,)), ((), ())),
        preferred_element_type=jnp.float32,
    )
    down_proj = head_sum(down_part, nhead)
    return (hidden_float + down_proj).astype(jnp.bfloat16).reshape(nsteps, requests, local_width)


def solution(mesh):
    placed = (
        P(None, None, "seq"),
        P(),
        P("seq"),
        P("seq"),
        P("seq", None, "head"),
        P("seq", None, "head"),
        P("head"),
        P("seq"),
        P("seq"),
        P("seq", None, "head"),
        P("seq", "head"),
        P("seq", "head"),
        P("seq", "head"),
    )
    nseq = mesh.shape["seq"]
    return jax.shard_map(
        functools.partial(on_device, nseq=nseq, nhead=mesh.shape["head"]), mesh=mesh, in_specs=placed, out_specs=P(None, None, "seq"), check_vma=False
    )
```

```python
import functools

import jax
import jax.numpy as jnp
from jax import lax
from jax.sharding import PartitionSpec as P

D = 4096
BLK = 8


eps_norm = 1e-05
floor_score = -1e30
highest = lax.Precision.HIGHEST


def normalize(token_rows, gain_share, totals, width_all):
    row_sum, row_squares = totals
    mean_value = row_sum / width_all
    variance = row_squares / width_all - mean_value * mean_value
    return (
        (token_rows.astype(jnp.float32) - mean_value[:, None])
        * lax.rsqrt(variance + eps_norm)[:, None]
        * gain_share[None, :]
    ).astype(jnp.bfloat16)


def page_block(carry_state, owners, number, key_block, value_block, queries, slopes, lengths):
    run_max, run_sum, run_out = carry_state
    nblock, page_len, width_all = key_block.shape
    nheads = slopes.shape[0]
    head_size = width_all // nheads
    nsteps, requests = queries.shape[0], queries.shape[1]
    safe_owner = jnp.clip(owners, 0, requests - 1)
    page_query = jnp.take(queries, safe_owner, axis=1)
    key_heads = key_block.reshape(nblock, page_len, nheads, head_size)
    value_heads = value_block.reshape(nblock, page_len, nheads, head_size)
    scores = jnp.einsum(
        "sbhe,bthe->sbth", page_query, key_heads, preferred_element_type=jnp.float32
    ) * head_size ** (-0.5)
    positions = number[:, None] * page_len + jnp.arange(page_len, dtype=jnp.int32)[None, :]
    own_length = jnp.take(lengths, safe_owner)
    step_ids = jnp.arange(nsteps, dtype=jnp.int32)
    distance = (
        own_length[None, :, None] + step_ids[:, None, None] - positions[None]
    ).astype(jnp.float32)
    scores = scores - distance[..., None] * slopes
    valid_mask = (owners[:, None] >= 0) & (positions < own_length[:, None])
    masked = jnp.where(valid_mask[None, :, :, None], scores, floor_score)
    page_max = jnp.max(masked, axis=2)
    member = owners[None, :] == jnp.arange(requests, dtype=jnp.int32)[:, None]
    block_max = jnp.max(
        jnp.where(member[None, :, :, None], page_max[:, None, :, :], floor_score), axis=2
    )
    next_max = jnp.maximum(run_max, block_max)
    owner_max = jnp.take(next_max, safe_owner, axis=1)
    expon = jnp.where(
        valid_mask[None, :, :, None], jnp.exp(masked - owner_max[:, :, None, :]), 0.0
    )
    page_sum = jnp.sum(expon, axis=2)
    weights = expon.astype(jnp.bfloat16)
    page_out = jnp.einsum(
        "sbth,bthe->sbhe", weights, value_heads, preferred_element_type=jnp.float32
    )
    member_float = member.astype(jnp.float32)
    rescale = jnp.exp(run_max - next_max)
    next_sum = run_sum * rescale + jnp.einsum(
        "rb,sbh->srh", member_float, page_sum, precision=highest
    )
    added = jnp.einsum(
        "rb,sbx->srx", member_float, page_out.reshape(nsteps, nblock, nheads * head_size),
        precision=highest,
    )
    next_out = run_out * rescale[..., None] + added.reshape(nsteps, requests, nheads, head_size)
    return (next_max, next_sum, next_out)


def attend_new(carry_state, queries, new_keys, new_values, slopes, token_step):
    run_max, run_sum, run_out = carry_state
    head_size = queries.shape[2]
    for earlier in range(token_step + 1):
        scores = jnp.sum(
            queries.astype(jnp.float32) * new_keys[earlier].astype(jnp.float32), axis=2
        ) * head_size ** (-0.5)
        scores = scores - slopes[None, :] * float(token_step - earlier)
        next_max = jnp.maximum(run_max, scores)
        rescale = jnp.exp(run_max - next_max)
        expon = jnp.exp(scores - next_max)
        weights = lax.optimization_barrier(expon.astype(jnp.bfloat16)).astype(jnp.float32)
        run_sum = run_sum * rescale + expon
        run_out = run_out * rescale[:, :, None] + weights[:, :, None] * new_values[earlier].astype(
            jnp.float32
        )
        run_max = next_max
    attended = (run_out / run_sum[:, :, None]).astype(jnp.bfloat16)
    return attended.reshape(attended.shape[0], -1)


def gather_rows(part, nseq):
    copies = jnp.broadcast_to(part[None], (nseq,) + part.shape)
    return lax.all_to_all(copies, "seq", 0, 0, tiled=True)


def gather_cols(part, nseq):
    got = gather_rows(part, nseq)
    return jnp.moveaxis(got, 0, -2).reshape(part.shape[:-1] + (nseq * part.shape[-1],))


def head_sum(part, nhead):
    my_index = lax.axis_index("head")
    stride = 1
    while stride < nhead:
        other = lax.ppermute(part, "head", [(i, i ^ stride) for i in range(nhead)])
        low = (my_index & stride) == 0
        part = jnp.where(low, part + other, other + part)
        stride *= 2
    return part


def full_normalize(rows, gain_full):
    row_float = rows.astype(jnp.float32)
    totals = (jnp.sum(row_float, axis=1), jnp.sum(row_float * row_float, axis=1))
    return normalize(rows, gain_full, totals, rows.shape[1])


def butterfly_combine(state, nseq):
    my_index = lax.axis_index("seq")
    stride = 1
    while stride < nseq:
        pairs = [(i, i ^ stride) for i in range(nseq)]
        other = lax.ppermute(state, "seq", pairs)
        low = (my_index & stride) == 0
        first = tuple(jnp.where(low, a, b) for a, b in zip(state, other))
        second = tuple(jnp.where(low, b, a) for a, b in zip(state, other))
        top = jnp.maximum(first[0], second[0])
        scale_a = jnp.exp(first[0] - top)
        scale_b = jnp.exp(second[0] - top)
        total = first[1] * scale_a + second[1] * scale_b
        out = first[2] * scale_a[:, :, None] + second[2] * scale_b[:, :, None]
        state = (top, total, out)
        stride *= 2
    return state


def attend_rows(carry_state, queries, new_keys, new_values, slopes, token_step):
    run_max, run_sum, run_out = carry_state
    head_size = queries.shape[2]
    for earlier in range(len(new_keys)):
        active = earlier <= token_step
        scores = jnp.sum(
            queries.astype(jnp.float32) * new_keys[earlier].astype(jnp.float32), axis=2
        ) * head_size ** (-0.5)
        scores = scores - slopes[None, :] * (token_step - earlier).astype(jnp.float32)
        next_max = jnp.maximum(run_max, scores)
        rescale = jnp.exp(run_max - next_max)
        expon = jnp.exp(scores - next_max)
        weights = lax.optimization_barrier(expon.astype(jnp.bfloat16)).astype(jnp.float32)
        next_sum = run_sum * rescale + expon
        next_out = run_out * rescale[:, :, None] + weights[:, :, None] * new_values[earlier].astype(
            jnp.float32
        )
        run_sum = jnp.where(active, next_sum, run_sum)
        run_out = jnp.where(active, next_out, run_out)
        run_max = jnp.where(active, next_max, run_max)
    attended = (run_out / run_sum[:, :, None]).astype(jnp.bfloat16)
    return attended.reshape(attended.shape[0], -1)


def on_device(
    tokens,
    lengths,
    page_owner,
    page_number,
    key_pages,
    value_pages,
    alibi_slopes,
    norm1_gain,
    norm2_gain,
    w_qkv,
    w_out,
    w_up,
    w_down,
    nseq,
    nhead,
):
    nsteps, requests, local_width = tokens.shape
    nheads = alibi_slopes.shape[0]
    head_width = key_pages.shape[2]
    head_size = head_width // nheads
    qkv_width = w_qkv.shape[1] * w_qkv.shape[2]
    rows = nsteps * requests

    qkv_chunk = qkv_width // nseq
    up_chunk = w_up.shape[1] // nseq
    gain_pair = jnp.stack([norm1_gain, norm2_gain])
    gain_parts = []
    for _ in range(3):
        piece = lax.optimization_barrier(gain_pair.astype(jnp.bfloat16))
        gain_parts.append(piece)
        gain_pair = gain_pair - piece.astype(jnp.float32)

    token_rows = tokens.reshape(rows, local_width)
    token_float = token_rows.astype(jnp.float32)
    pad_width = max(local_width, qkv_chunk, up_chunk)
    head_rows = -(-(rows + 6) // 16) * 16

    def lanes(block):
        return jnp.pad(block, [(0, 0)] * (block.ndim - 1) + [(0, pad_width - block.shape[-1])])

    token_pack = jnp.concatenate([token_rows] + gain_parts, axis=0)
    token_pack = jnp.pad(lanes(token_pack), ((0, head_rows - rows - 6), (0, 0)))
    payload = jnp.concatenate(
        [
            jnp.broadcast_to(token_pack[None], (nseq,) + token_pack.shape),
            lanes(jnp.swapaxes(w_qkv.reshape(local_width, nseq, qkv_chunk), 0, 1)),
            lanes(jnp.swapaxes(w_up.reshape(local_width, nseq, up_chunk), 0, 1)),
        ],
        axis=1,
    )
    got = lax.all_to_all(payload, "seq", 0, 0, tiled=True)
    gathered = jnp.moveaxis(got[:, : rows + 6, :local_width], 0, -2).reshape(rows + 6, nseq * local_width)
    qkv_cols = got[:, head_rows : head_rows + local_width, :qkv_chunk].reshape(nseq * local_width, qkv_chunk)
    up_cols = got[:, head_rows + local_width :, :up_chunk].reshape(nseq * local_width, up_chunk)
    pieces = gathered[rows:].astype(jnp.float32)
    gains = (pieces[0:2] + pieces[2:4]) + pieces[4:6]
    normed = full_normalize(gathered[:rows], gains[0])
    qkv_part = jnp.dot(normed, qkv_cols, preferred_element_type=jnp.float32).astype(jnp.bfloat16)
    joined = gather_cols(qkv_part, nseq)
    all_queries = joined[:, :head_width].reshape(nsteps, requests, nheads, head_size)
    new_keys = joined[:, head_width : 2 * head_width].reshape(nsteps, requests, nheads, head_size)
    new_values = joined[:, 2 * head_width :].reshape(nsteps, requests, nheads, head_size)

    carry_state = (
        jnp.full((nsteps, requests, nheads), floor_score, jnp.float32),
        jnp.zeros((nsteps, requests, nheads), jnp.float32),
        jnp.zeros((nsteps, requests, nheads, head_size), jnp.float32),
    )

    final_state = page_block(
        carry_state, page_owner, page_number, key_pages, value_pages, all_queries, alibi_slopes, lengths
    )

    joined_state = tuple(part.reshape((rows,) + part.shape[2:]) for part in final_state)
    run_max, run_sum, run_out = joined_state
    own_rows = rows // nseq
    stats = jnp.concatenate(
        [
            jnp.swapaxes(run_max.reshape(nseq, own_rows, nheads), 1, 2),
            jnp.swapaxes(run_sum.reshape(nseq, own_rows, nheads), 1, 2),
            jnp.zeros((nseq, nheads, head_size - 2 * own_rows), jnp.float32),
        ],
        axis=2,
    )
    packed = jnp.concatenate(
        [run_out.reshape(nseq, own_rows, nheads, head_size), stats[:, None]], axis=1
    )
    packed = lax.all_to_all(packed, "seq", 0, 0, tiled=True)
    part_out = packed[:, :own_rows]
    part_max = jnp.swapaxes(packed[:, own_rows, :, :own_rows], 1, 2)
    part_sum = jnp.swapaxes(packed[:, own_rows, :, own_rows : 2 * own_rows], 1, 2)
    top_max = jnp.max(part_max, axis=0)
    rescale = jnp.exp(part_max - top_max[None])
    top_sum = jnp.sum(part_sum * rescale, axis=0)
    top_out = jnp.sum(part_out * rescale[:, :, :, None], axis=0)
    first_row = lax.axis_index("seq") * own_rows
    my_step = first_row // requests
    pick = lambda a: lax.dynamic_slice_in_dim(a.reshape(rows, nheads, head_size), first_row, own_rows, 0)
    my_queries = pick(all_queries)
    my_keys = []
    my_values = []
    for earlier in range(nsteps):
        shifted = first_row - (my_step - earlier) * requests
        my_keys.append(lax.dynamic_slice_in_dim(new_keys.reshape(rows, nheads, head_size), shifted, own_rows, 0))
        my_values.append(lax.dynamic_slice_in_dim(new_values.reshape(rows, nheads, head_size), shifted, own_rows, 0))
    mine = attend_rows(
        (top_max, top_sum, top_out), my_queries, my_keys, my_values, alibi_slopes, my_step
    )
    attended = gather_rows(mine, nseq).reshape(rows, -1)
    projected = head_sum(
        lax.dot_general(attended, w_out, (((1,), (1,)), ((), ())), preferred_element_type=jnp.float32),
        nhead,
    )
    hidden_in = (token_float + projected).astype(jnp.bfloat16)
    hidden_float = hidden_in.astype(jnp.float32)
    normed_two = full_normalize(gather_cols(hidden_in, nseq), gains[1])
    up_share = jnp.dot(normed_two, up_cols, preferred_element_type=jnp.float32)
    hidden_share = jax.nn.gelu(up_share, approximate=False).astype(jnp.bfloat16)
    down_part = lax.dot_general(
        gather_cols(hidden_share, nseq),
        w_down,
        (((1,), (1,)), ((), ())),
        preferred_element_type=jnp.float32,
    )
    down_proj = head_sum(down_part, nhead)
    return (hidden_float + down_proj).astype(jnp.bfloat16).reshape(nsteps, requests, local_width)


def solution(mesh):
    placed = (
        P(None, None, "seq"),
        P(),
        P("seq"),
        P("seq"),
        P("seq", None, "head"),
        P("seq", None, "head"),
        P("head"),
        P("seq"),
        P("seq"),
        P("seq", None, "head"),
        P("seq", "head"),
        P("seq", "head"),
        P("seq", "head"),
    )
    nseq = mesh.shape["seq"]
    return jax.shard_map(
        functools.partial(on_device, nseq=nseq, nhead=mesh.shape["head"]), mesh=mesh, in_specs=placed, out_specs=P(None, None, "seq"), check_vma=False
    )
```

```python
import functools

import jax
import jax.numpy as jnp
from jax import lax
from jax.sharding import PartitionSpec as P

D = 4096
BLK = 8


eps_norm = 1e-05
floor_score = -1e30
highest = lax.Precision.HIGHEST


def normalize(token_rows, gain_share, totals, width_all):
    row_sum, row_squares = totals
    mean_value = row_sum / width_all
    variance = row_squares / width_all - mean_value * mean_value
    return (
        (token_rows.astype(jnp.float32) - mean_value[:, None])
        * lax.rsqrt(variance + eps_norm)[:, None]
        * gain_share[None, :]
    ).astype(jnp.bfloat16)


def page_block(carry_state, owners, number, key_block, value_block, queries, slopes, lengths):
    run_max, run_sum, run_out = carry_state
    nblock, page_len, width_all = key_block.shape
    nheads = slopes.shape[0]
    head_size = width_all // nheads
    nsteps, requests = queries.shape[0], queries.shape[1]
    safe_owner = jnp.clip(owners, 0, requests - 1)
    page_query = jnp.take(queries, safe_owner, axis=1)
    key_heads = key_block.reshape(nblock, page_len, nheads, head_size)
    value_heads = value_block.reshape(nblock, page_len, nheads, head_size)
    scores = jnp.einsum(
        "sbhe,bthe->sbth", page_query, key_heads, preferred_element_type=jnp.float32
    ) * head_size ** (-0.5)
    positions = number[:, None] * page_len + jnp.arange(page_len, dtype=jnp.int32)[None, :]
    own_length = jnp.take(lengths, safe_owner)
    step_ids = jnp.arange(nsteps, dtype=jnp.int32)
    distance = (
        own_length[None, :, None] + step_ids[:, None, None] - positions[None]
    ).astype(jnp.float32)
    scores = scores - distance[..., None] * slopes
    valid_mask = (owners[:, None] >= 0) & (positions < own_length[:, None])
    masked = jnp.where(valid_mask[None, :, :, None], scores, floor_score)
    page_max = jnp.max(masked, axis=2)
    member = owners[None, :] == jnp.arange(requests, dtype=jnp.int32)[:, None]
    block_max = jnp.max(
        jnp.where(member[None, :, :, None], page_max[:, None, :, :], floor_score), axis=2
    )
    next_max = jnp.maximum(run_max, block_max)
    owner_max = jnp.take(next_max, safe_owner, axis=1)
    expon = jnp.where(
        valid_mask[None, :, :, None], jnp.exp(masked - owner_max[:, :, None, :]), 0.0
    )
    page_sum = jnp.sum(expon, axis=2)
    weights = expon.astype(jnp.bfloat16)
    page_out = jnp.einsum(
        "sbth,bthe->sbhe", weights, value_heads, preferred_element_type=jnp.float32
    )
    member_float = member.astype(jnp.float32)
    rescale = jnp.exp(run_max - next_max)
    next_sum = run_sum * rescale + jnp.einsum(
        "rb,sbh->srh", member_float, page_sum, precision=highest
    )
    added = jnp.einsum(
        "rb,sbx->srx", member_float, page_out.reshape(nsteps, nblock, nheads * head_size),
        precision=highest,
    )
    next_out = run_out * rescale[..., None] + added.reshape(nsteps, requests, nheads, head_size)
    return (next_max, next_sum, next_out)


def attend_new(carry_state, queries, new_keys, new_values, slopes, token_step):
    run_max, run_sum, run_out = carry_state
    head_size = queries.shape[2]
    for earlier in range(token_step + 1):
        scores = jnp.sum(
            queries.astype(jnp.float32) * new_keys[earlier].astype(jnp.float32), axis=2
        ) * head_size ** (-0.5)
        scores = scores - slopes[None, :] * float(token_step - earlier)
        next_max = jnp.maximum(run_max, scores)
        rescale = jnp.exp(run_max - next_max)
        expon = jnp.exp(scores - next_max)
        weights = lax.optimization_barrier(expon.astype(jnp.bfloat16)).astype(jnp.float32)
        run_sum = run_sum * rescale + expon
        run_out = run_out * rescale[:, :, None] + weights[:, :, None] * new_values[earlier].astype(
            jnp.float32
        )
        run_max = next_max
    attended = (run_out / run_sum[:, :, None]).astype(jnp.bfloat16)
    return attended.reshape(attended.shape[0], -1)


def gather_rows(part, nseq):
    copies = jnp.broadcast_to(part[None], (nseq,) + part.shape)
    return lax.all_to_all(copies, "seq", 0, 0, tiled=True)


def gather_cols(part, nseq):
    got = gather_rows(part, nseq)
    return jnp.moveaxis(got, 0, -2).reshape(part.shape[:-1] + (nseq * part.shape[-1],))


def head_sum(part, nhead):
    my_index = lax.axis_index("head")
    stride = 1
    while stride < nhead:
        other = lax.ppermute(part, "head", [(i, i ^ stride) for i in range(nhead)])
        low = (my_index & stride) == 0
        part = jnp.where(low, part + other, other + part)
        stride *= 2
    return part


def full_normalize(rows, gain_full):
    row_float = rows.astype(jnp.float32)
    totals = (jnp.sum(row_float, axis=1), jnp.sum(row_float * row_float, axis=1))
    return normalize(rows, gain_full, totals, rows.shape[1])


def butterfly_combine(state, nseq):
    my_index = lax.axis_index("seq")
    stride = 1
    while stride < nseq:
        pairs = [(i, i ^ stride) for i in range(nseq)]
        other = lax.ppermute(state, "seq", pairs)
        low = (my_index & stride) == 0
        first = tuple(jnp.where(low, a, b) for a, b in zip(state, other))
        second = tuple(jnp.where(low, b, a) for a, b in zip(state, other))
        top = jnp.maximum(first[0], second[0])
        scale_a = jnp.exp(first[0] - top)
        scale_b = jnp.exp(second[0] - top)
        total = first[1] * scale_a + second[1] * scale_b
        out = first[2] * scale_a[:, :, None] + second[2] * scale_b[:, :, None]
        state = (top, total, out)
        stride *= 2
    return state


def attend_rows(carry_state, queries, new_keys, new_values, slopes, token_step):
    run_max, run_sum, run_out = carry_state
    head_size = queries.shape[2]
    for earlier in range(len(new_keys)):
        active = earlier <= token_step
        scores = jnp.sum(
            queries.astype(jnp.float32) * new_keys[earlier].astype(jnp.float32), axis=2
        ) * head_size ** (-0.5)
        scores = scores - slopes[None, :] * (token_step - earlier).astype(jnp.float32)
        next_max = jnp.maximum(run_max, scores)
        rescale = jnp.exp(run_max - next_max)
        expon = jnp.exp(scores - next_max)
        weights = lax.optimization_barrier(expon.astype(jnp.bfloat16)).astype(jnp.float32)
        next_sum = run_sum * rescale + expon
        next_out = run_out * rescale[:, :, None] + weights[:, :, None] * new_values[earlier].astype(
            jnp.float32
        )
        run_sum = jnp.where(active, next_sum, run_sum)
        run_out = jnp.where(active, next_out, run_out)
        run_max = jnp.where(active, next_max, run_max)
    attended = (run_out / run_sum[:, :, None]).astype(jnp.bfloat16)
    return attended.reshape(attended.shape[0], -1)


def on_device(
    tokens,
    lengths,
    page_owner,
    page_number,
    key_pages,
    value_pages,
    alibi_slopes,
    norm1_gain,
    norm2_gain,
    w_qkv,
    w_out,
    w_up,
    w_down,
    nseq,
    nhead,
):
    nsteps, requests, local_width = tokens.shape
    nheads = alibi_slopes.shape[0]
    head_width = key_pages.shape[2]
    head_size = head_width // nheads
    qkv_width = w_qkv.shape[1] * w_qkv.shape[2]
    rows = nsteps * requests

    qkv_chunk = qkv_width // nseq
    up_chunk = w_up.shape[1] // nseq
    gain_pair = jnp.stack([norm1_gain, norm2_gain])
    gain_parts = []
    for _ in range(3):
        piece = lax.optimization_barrier(gain_pair.astype(jnp.bfloat16))
        gain_parts.append(piece)
        gain_pair = gain_pair - piece.astype(jnp.float32)

    token_rows = tokens.reshape(rows, local_width)
    token_float = token_rows.astype(jnp.float32)
    pad_width = max(local_width, qkv_chunk + 6, up_chunk)

    def lanes(block):
        return jnp.pad(block, [(0, 0)] * (block.ndim - 1) + [(0, pad_width - block.shape[-1])])

    gain_cols = jnp.concatenate(gain_parts, axis=0).T
    qkv_block = jnp.swapaxes(w_qkv.reshape(local_width, nseq, qkv_chunk), 0, 1)
    qkv_block = jnp.concatenate(
        [qkv_block, jnp.broadcast_to(gain_cols[None], (nseq,) + gain_cols.shape)], axis=2
    )
    payload = jnp.concatenate(
        [
            jnp.broadcast_to(lanes(token_rows)[None], (nseq, rows, pad_width)),
            lanes(qkv_block),
            lanes(jnp.swapaxes(w_up.reshape(local_width, nseq, up_chunk), 0, 1)),
        ],
        axis=1,
    )
    got = lax.all_to_all(payload, "seq", 0, 0, tiled=True)
    gathered = jnp.moveaxis(got[:, :rows, :local_width], 0, -2).reshape(rows, nseq * local_width)
    qkv_got = got[:, rows : rows + local_width]
    qkv_cols = qkv_got[:, :, :qkv_chunk].reshape(nseq * local_width, qkv_chunk)
    pieces = qkv_got[:, :, qkv_chunk : qkv_chunk + 6].reshape(nseq * local_width, 6).T.astype(jnp.float32)
    up_cols = got[:, rows + local_width :, :up_chunk].reshape(nseq * local_width, up_chunk)
    gains = (pieces[0:2] + pieces[2:4]) + pieces[4:6]
    normed = full_normalize(gathered, gains[0])
    qkv_part = jnp.dot(normed, qkv_cols, preferred_element_type=jnp.float32).astype(jnp.bfloat16)
    joined = gather_cols(qkv_part, nseq)
    all_queries = joined[:, :head_width].reshape(nsteps, requests, nheads, head_size)
    new_keys = joined[:, head_width : 2 * head_width].reshape(nsteps, requests, nheads, head_size)
    new_values = joined[:, 2 * head_width :].reshape(nsteps, requests, nheads, head_size)

    carry_state = (
        jnp.full((nsteps, requests, nheads), floor_score, jnp.float32),
        jnp.zeros((nsteps, requests, nheads), jnp.float32),
        jnp.zeros((nsteps, requests, nheads, head_size), jnp.float32),
    )

    final_state = page_block(
        carry_state, page_owner, page_number, key_pages, value_pages, all_queries, alibi_slopes, lengths
    )

    joined_state = tuple(part.reshape((rows,) + part.shape[2:]) for part in final_state)
    run_max, run_sum, run_out = joined_state
    own_rows = rows // nseq
    stats = jnp.concatenate(
        [
            jnp.swapaxes(run_max.reshape(nseq, own_rows, nheads), 1, 2),
            jnp.swapaxes(run_sum.reshape(nseq, own_rows, nheads), 1, 2),
            jnp.zeros((nseq, nheads, head_size - 2 * own_rows), jnp.float32),
        ],
        axis=2,
    )
    packed = jnp.concatenate(
        [run_out.reshape(nseq, own_rows, nheads, head_size), stats[:, None]], axis=1
    )
    packed = lax.all_to_all(packed, "seq", 0, 0, tiled=True)
    part_out = packed[:, :own_rows]
    part_max = jnp.swapaxes(packed[:, own_rows, :, :own_rows], 1, 2)
    part_sum = jnp.swapaxes(packed[:, own_rows, :, own_rows : 2 * own_rows], 1, 2)
    top_max = jnp.max(part_max, axis=0)
    rescale = jnp.exp(part_max - top_max[None])
    top_sum = jnp.sum(part_sum * rescale, axis=0)
    top_out = jnp.sum(part_out * rescale[:, :, :, None], axis=0)
    first_row = lax.axis_index("seq") * own_rows
    my_step = first_row // requests
    pick = lambda a: lax.dynamic_slice_in_dim(a.reshape(rows, nheads, head_size), first_row, own_rows, 0)
    my_queries = pick(all_queries)
    my_keys = []
    my_values = []
    for earlier in range(nsteps):
        shifted = first_row - (my_step - earlier) * requests
        my_keys.append(lax.dynamic_slice_in_dim(new_keys.reshape(rows, nheads, head_size), shifted, own_rows, 0))
        my_values.append(lax.dynamic_slice_in_dim(new_values.reshape(rows, nheads, head_size), shifted, own_rows, 0))
    mine = attend_rows(
        (top_max, top_sum, top_out), my_queries, my_keys, my_values, alibi_slopes, my_step
    )
    attended = gather_rows(mine, nseq).reshape(rows, -1)
    projected = head_sum(
        lax.dot_general(attended, w_out, (((1,), (1,)), ((), ())), preferred_element_type=jnp.float32),
        nhead,
    )
    hidden_in = (token_float + projected).astype(jnp.bfloat16)
    hidden_float = hidden_in.astype(jnp.float32)
    normed_two = full_normalize(gather_cols(hidden_in, nseq), gains[1])
    up_share = jnp.dot(normed_two, up_cols, preferred_element_type=jnp.float32)
    hidden_share = jax.nn.gelu(up_share, approximate=False).astype(jnp.bfloat16)
    down_part = lax.dot_general(
        gather_cols(hidden_share, nseq),
        w_down,
        (((1,), (1,)), ((), ())),
        preferred_element_type=jnp.float32,
    )
    down_proj = head_sum(down_part, nhead)
    return (hidden_float + down_proj).astype(jnp.bfloat16).reshape(nsteps, requests, local_width)


def solution(mesh):
    placed = (
        P(None, None, "seq"),
        P(),
        P("seq"),
        P("seq"),
        P("seq", None, "head"),
        P("seq", None, "head"),
        P("head"),
        P("seq"),
        P("seq"),
        P("seq", None, "head"),
        P("seq", "head"),
        P("seq", "head"),
        P("seq", "head"),
    )
    nseq = mesh.shape["seq"]
    return jax.shard_map(
        functools.partial(on_device, nseq=nseq, nhead=mesh.shape["head"]), mesh=mesh, in_specs=placed, out_specs=P(None, None, "seq"), check_vma=False
    )
```

```python
import functools

import jax
import jax.numpy as jnp
from jax import lax
from jax.sharding import PartitionSpec as P

D = 4096
BLK = 8


eps_norm = 1e-05
floor_score = -1e30
highest = lax.Precision.HIGHEST


def normalize(token_rows, gain_share, totals, width_all):
    row_sum, row_squares = totals
    mean_value = row_sum / width_all
    variance = row_squares / width_all - mean_value * mean_value
    return (
        (token_rows.astype(jnp.float32) - mean_value[:, None])
        * lax.rsqrt(variance + eps_norm)[:, None]
        * gain_share[None, :]
    ).astype(jnp.bfloat16)


def page_block(carry_state, owners, number, key_block, value_block, queries, slopes, lengths):
    run_max, run_sum, run_out = carry_state
    nblock, page_len, width_all = key_block.shape
    nheads = slopes.shape[0]
    head_size = width_all // nheads
    nsteps, requests = queries.shape[0], queries.shape[1]
    safe_owner = jnp.clip(owners, 0, requests - 1)
    page_query = jnp.take(queries, safe_owner, axis=1)
    key_heads = key_block.reshape(nblock, page_len, nheads, head_size)
    value_heads = value_block.reshape(nblock, page_len, nheads, head_size)
    scores = jnp.einsum(
        "sbhe,bthe->sbth", page_query, key_heads, preferred_element_type=jnp.float32
    ) * head_size ** (-0.5)
    positions = number[:, None] * page_len + jnp.arange(page_len, dtype=jnp.int32)[None, :]
    own_length = jnp.take(lengths, safe_owner)
    step_ids = jnp.arange(nsteps, dtype=jnp.int32)
    distance = (
        own_length[None, :, None] + step_ids[:, None, None] - positions[None]
    ).astype(jnp.float32)
    scores = scores - distance[..., None] * slopes
    valid_mask = (owners[:, None] >= 0) & (positions < own_length[:, None])
    masked = jnp.where(valid_mask[None, :, :, None], scores, floor_score)
    page_max = jnp.max(masked, axis=2)
    member = owners[None, :] == jnp.arange(requests, dtype=jnp.int32)[:, None]
    block_max = jnp.max(
        jnp.where(member[None, :, :, None], page_max[:, None, :, :], floor_score), axis=2
    )
    next_max = jnp.maximum(run_max, block_max)
    owner_max = jnp.take(next_max, safe_owner, axis=1)
    expon = jnp.where(
        valid_mask[None, :, :, None], jnp.exp(masked - owner_max[:, :, None, :]), 0.0
    )
    page_sum = jnp.sum(expon, axis=2)
    weights = expon.astype(jnp.bfloat16)
    page_out = jnp.einsum(
        "sbth,bthe->sbhe", weights, value_heads, preferred_element_type=jnp.float32
    )
    member_float = member.astype(jnp.float32)
    rescale = jnp.exp(run_max - next_max)
    next_sum = run_sum * rescale + jnp.einsum(
        "rb,sbh->srh", member_float, page_sum, precision=highest
    )
    added = jnp.einsum(
        "rb,sbx->srx", member_float, page_out.reshape(nsteps, nblock, nheads * head_size),
        precision=highest,
    )
    next_out = run_out * rescale[..., None] + added.reshape(nsteps, requests, nheads, head_size)
    return (next_max, next_sum, next_out)


def attend_new(carry_state, queries, new_keys, new_values, slopes, token_step):
    run_max, run_sum, run_out = carry_state
    head_size = queries.shape[2]
    for earlier in range(token_step + 1):
        scores = jnp.sum(
            queries.astype(jnp.float32) * new_keys[earlier].astype(jnp.float32), axis=2
        ) * head_size ** (-0.5)
        scores = scores - slopes[None, :] * float(token_step - earlier)
        next_max = jnp.maximum(run_max, scores)
        rescale = jnp.exp(run_max - next_max)
        expon = jnp.exp(scores - next_max)
        weights = lax.optimization_barrier(expon.astype(jnp.bfloat16)).astype(jnp.float32)
        run_sum = run_sum * rescale + expon
        run_out = run_out * rescale[:, :, None] + weights[:, :, None] * new_values[earlier].astype(
            jnp.float32
        )
        run_max = next_max
    attended = (run_out / run_sum[:, :, None]).astype(jnp.bfloat16)
    return attended.reshape(attended.shape[0], -1)


def gather_rows(part, nseq):
    copies = jnp.broadcast_to(part[None], (nseq,) + part.shape)
    return lax.all_to_all(copies, "seq", 0, 0, tiled=True)


def gather_cols(part, nseq):
    got = gather_rows(part, nseq)
    return jnp.moveaxis(got, 0, -2).reshape(part.shape[:-1] + (nseq * part.shape[-1],))


def head_sum(part, nhead):
    copies = jnp.broadcast_to(part[None], (nhead,) + part.shape)
    got = lax.all_to_all(copies, "head", 0, 0, tiled=True)
    while got.shape[0] > 1:
        half = got.shape[0] // 2
        got = got[:half] + got[half:]
    return got[0]


def full_normalize(rows, gain_full):
    row_float = rows.astype(jnp.float32)
    totals = (jnp.sum(row_float, axis=1), jnp.sum(row_float * row_float, axis=1))
    return normalize(rows, gain_full, totals, rows.shape[1])


def butterfly_combine(state, nseq):
    my_index = lax.axis_index("seq")
    stride = 1
    while stride < nseq:
        pairs = [(i, i ^ stride) for i in range(nseq)]
        other = lax.ppermute(state, "seq", pairs)
        low = (my_index & stride) == 0
        first = tuple(jnp.where(low, a, b) for a, b in zip(state, other))
        second = tuple(jnp.where(low, b, a) for a, b in zip(state, other))
        top = jnp.maximum(first[0], second[0])
        scale_a = jnp.exp(first[0] - top)
        scale_b = jnp.exp(second[0] - top)
        total = first[1] * scale_a + second[1] * scale_b
        out = first[2] * scale_a[:, :, None] + second[2] * scale_b[:, :, None]
        state = (top, total, out)
        stride *= 2
    return state


def attend_rows(carry_state, queries, new_keys, new_values, slopes, token_step):
    run_max, run_sum, run_out = carry_state
    head_size = queries.shape[2]
    for earlier in range(len(new_keys)):
        active = earlier <= token_step
        scores = jnp.sum(
            queries.astype(jnp.float32) * new_keys[earlier].astype(jnp.float32), axis=2
        ) * head_size ** (-0.5)
        scores = scores - slopes[None, :] * (token_step - earlier).astype(jnp.float32)
        next_max = jnp.maximum(run_max, scores)
        rescale = jnp.exp(run_max - next_max)
        expon = jnp.exp(scores - next_max)
        weights = lax.optimization_barrier(expon.astype(jnp.bfloat16)).astype(jnp.float32)
        next_sum = run_sum * rescale + expon
        next_out = run_out * rescale[:, :, None] + weights[:, :, None] * new_values[earlier].astype(
            jnp.float32
        )
        run_sum = jnp.where(active, next_sum, run_sum)
        run_out = jnp.where(active, next_out, run_out)
        run_max = jnp.where(active, next_max, run_max)
    attended = (run_out / run_sum[:, :, None]).astype(jnp.bfloat16)
    return attended.reshape(attended.shape[0], -1)


def on_device(
    tokens,
    lengths,
    page_owner,
    page_number,
    key_pages,
    value_pages,
    alibi_slopes,
    norm1_gain,
    norm2_gain,
    w_qkv,
    w_out,
    w_up,
    w_down,
    nseq,
    nhead,
):
    nsteps, requests, local_width = tokens.shape
    nheads = alibi_slopes.shape[0]
    head_width = key_pages.shape[2]
    head_size = head_width // nheads
    qkv_width = w_qkv.shape[1] * w_qkv.shape[2]
    rows = nsteps * requests

    qkv_chunk = qkv_width // nseq
    up_chunk = w_up.shape[1] // nseq
    gain_pair = jnp.stack([norm1_gain, norm2_gain])
    gain_parts = []
    for _ in range(3):
        piece = lax.optimization_barrier(gain_pair.astype(jnp.bfloat16))
        gain_parts.append(piece)
        gain_pair = gain_pair - piece.astype(jnp.float32)

    token_rows = tokens.reshape(rows, local_width)
    token_float = token_rows.astype(jnp.float32)
    pad_width = max(local_width, qkv_chunk + 6, up_chunk)

    def lanes(block):
        return jnp.pad(block, [(0, 0)] * (block.ndim - 1) + [(0, pad_width - block.shape[-1])])

    gain_cols = jnp.concatenate(gain_parts, axis=0).T
    qkv_block = jnp.swapaxes(w_qkv.reshape(local_width, nseq, qkv_chunk), 0, 1)
    qkv_block = jnp.concatenate(
        [qkv_block, jnp.broadcast_to(gain_cols[None], (nseq,) + gain_cols.shape)], axis=2
    )
    payload = jnp.concatenate(
        [
            jnp.broadcast_to(lanes(token_rows)[None], (nseq, rows, pad_width)),
            lanes(qkv_block),
            lanes(jnp.swapaxes(w_up.reshape(local_width, nseq, up_chunk), 0, 1)),
        ],
        axis=1,
    )
    got = lax.all_to_all(payload, "seq", 0, 0, tiled=True)
    gathered = jnp.moveaxis(got[:, :rows, :local_width], 0, -2).reshape(rows, nseq * local_width)
    qkv_got = got[:, rows : rows + local_width]
    qkv_cols = qkv_got[:, :, :qkv_chunk].reshape(nseq * local_width, qkv_chunk)
    pieces = qkv_got[:, :, qkv_chunk : qkv_chunk + 6].reshape(nseq * local_width, 6).T.astype(jnp.float32)
    up_cols = got[:, rows + local_width :, :up_chunk].reshape(nseq * local_width, up_chunk)
    gains = (pieces[0:2] + pieces[2:4]) + pieces[4:6]
    normed = full_normalize(gathered, gains[0])
    qkv_part = jnp.dot(normed, qkv_cols, preferred_element_type=jnp.float32).astype(jnp.bfloat16)
    joined = gather_cols(qkv_part, nseq)
    all_queries = joined[:, :head_width].reshape(nsteps, requests, nheads, head_size)
    new_keys = joined[:, head_width : 2 * head_width].reshape(nsteps, requests, nheads, head_size)
    new_values = joined[:, 2 * head_width :].reshape(nsteps, requests, nheads, head_size)

    carry_state = (
        jnp.full((nsteps, requests, nheads), floor_score, jnp.float32),
        jnp.zeros((nsteps, requests, nheads), jnp.float32),
        jnp.zeros((nsteps, requests, nheads, head_size), jnp.float32),
    )

    final_state = page_block(
        carry_state, page_owner, page_number, key_pages, value_pages, all_queries, alibi_slopes, lengths
    )

    joined_state = tuple(part.reshape((rows,) + part.shape[2:]) for part in final_state)
    run_max, run_sum, run_out = joined_state
    own_rows = rows // nseq
    stats = jnp.concatenate(
        [
            jnp.swapaxes(run_max.reshape(nseq, own_rows, nheads), 1, 2),
            jnp.swapaxes(run_sum.reshape(nseq, own_rows, nheads), 1, 2),
            jnp.zeros((nseq, nheads, head_size - 2 * own_rows), jnp.float32),
        ],
        axis=2,
    )
    packed = jnp.concatenate(
        [run_out.reshape(nseq, own_rows, nheads, head_size), stats[:, None]], axis=1
    )
    packed = lax.all_to_all(packed, "seq", 0, 0, tiled=True)
    part_out = packed[:, :own_rows]
    part_max = jnp.swapaxes(packed[:, own_rows, :, :own_rows], 1, 2)
    part_sum = jnp.swapaxes(packed[:, own_rows, :, own_rows : 2 * own_rows], 1, 2)
    top_max = jnp.max(part_max, axis=0)
    rescale = jnp.exp(part_max - top_max[None])
    top_sum = jnp.sum(part_sum * rescale, axis=0)
    top_out = jnp.sum(part_out * rescale[:, :, :, None], axis=0)
    first_row = lax.axis_index("seq") * own_rows
    my_step = first_row // requests
    pick = lambda a: lax.dynamic_slice_in_dim(a.reshape(rows, nheads, head_size), first_row, own_rows, 0)
    my_queries = pick(all_queries)
    my_keys = []
    my_values = []
    for earlier in range(nsteps):
        shifted = first_row - (my_step - earlier) * requests
        my_keys.append(lax.dynamic_slice_in_dim(new_keys.reshape(rows, nheads, head_size), shifted, own_rows, 0))
        my_values.append(lax.dynamic_slice_in_dim(new_values.reshape(rows, nheads, head_size), shifted, own_rows, 0))
    mine = attend_rows(
        (top_max, top_sum, top_out), my_queries, my_keys, my_values, alibi_slopes, my_step
    )
    attended = gather_rows(mine, nseq).reshape(rows, -1)
    projected = head_sum(
        lax.dot_general(attended, w_out, (((1,), (1,)), ((), ())), preferred_element_type=jnp.float32),
        nhead,
    )
    hidden_in = (token_float + projected).astype(jnp.bfloat16)
    hidden_float = hidden_in.astype(jnp.float32)
    normed_two = full_normalize(gather_cols(hidden_in, nseq), gains[1])
    up_share = jnp.dot(normed_two, up_cols, preferred_element_type=jnp.float32)
    hidden_share = jax.nn.gelu(up_share, approximate=False).astype(jnp.bfloat16)
    down_part = lax.dot_general(
        gather_cols(hidden_share, nseq),
        w_down,
        (((1,), (1,)), ((), ())),
        preferred_element_type=jnp.float32,
    )
    down_proj = head_sum(down_part, nhead)
    return (hidden_float + down_proj).astype(jnp.bfloat16).reshape(nsteps, requests, local_width)


def solution(mesh):
    placed = (
        P(None, None, "seq"),
        P(),
        P("seq"),
        P("seq"),
        P("seq", None, "head"),
        P("seq", None, "head"),
        P("head"),
        P("seq"),
        P("seq"),
        P("seq", None, "head"),
        P("seq", "head"),
        P("seq", "head"),
        P("seq", "head"),
    )
    nseq = mesh.shape["seq"]
    return jax.shard_map(
        functools.partial(on_device, nseq=nseq, nhead=mesh.shape["head"]), mesh=mesh, in_specs=placed, out_specs=P(None, None, "seq"), check_vma=False
    )
```

```python
import functools

import jax
import jax.numpy as jnp
from jax import lax
from jax.sharding import PartitionSpec as P

D = 4096
BLK = 8


eps_norm = 1e-05
floor_score = -1e30
highest = lax.Precision.HIGHEST


def normalize(token_rows, gain_share, totals, width_all):
    row_sum, row_squares = totals
    mean_value = row_sum / width_all
    variance = row_squares / width_all - mean_value * mean_value
    return (
        (token_rows.astype(jnp.float32) - mean_value[:, None])
        * lax.rsqrt(variance + eps_norm)[:, None]
        * gain_share[None, :]
    ).astype(jnp.bfloat16)


def page_block(carry_state, owners, number, key_block, value_block, queries, slopes, lengths):
    run_max, run_sum, run_out = carry_state
    nblock, page_len, width_all = key_block.shape
    nheads = slopes.shape[0]
    head_size = width_all // nheads
    nsteps, requests = queries.shape[0], queries.shape[1]
    safe_owner = jnp.clip(owners, 0, requests - 1)
    page_query = jnp.take(queries, safe_owner, axis=1)
    key_heads = key_block.reshape(nblock, page_len, nheads, head_size)
    value_heads = value_block.reshape(nblock, page_len, nheads, head_size)
    scores = jnp.einsum(
        "sbhe,bthe->sbth", page_query, key_heads, preferred_element_type=jnp.float32
    ) * head_size ** (-0.5)
    positions = number[:, None] * page_len + jnp.arange(page_len, dtype=jnp.int32)[None, :]
    own_length = jnp.take(lengths, safe_owner)
    step_ids = jnp.arange(nsteps, dtype=jnp.int32)
    distance = (
        own_length[None, :, None] + step_ids[:, None, None] - positions[None]
    ).astype(jnp.float32)
    scores = scores - distance[..., None] * slopes
    valid_mask = (owners[:, None] >= 0) & (positions < own_length[:, None])
    masked = jnp.where(valid_mask[None, :, :, None], scores, floor_score)
    page_max = jnp.max(masked, axis=2)
    member = owners[None, :] == jnp.arange(requests, dtype=jnp.int32)[:, None]
    block_max = jnp.max(
        jnp.where(member[None, :, :, None], page_max[:, None, :, :], floor_score), axis=2
    )
    next_max = jnp.maximum(run_max, block_max)
    owner_max = jnp.take(next_max, safe_owner, axis=1)
    expon = jnp.where(
        valid_mask[None, :, :, None], jnp.exp(masked - owner_max[:, :, None, :]), 0.0
    )
    page_sum = jnp.sum(expon, axis=2)
    weights = expon.astype(jnp.bfloat16)
    page_out = jnp.einsum(
        "sbth,bthe->sbhe", weights, value_heads, preferred_element_type=jnp.float32
    )
    member_float = member.astype(jnp.float32)
    rescale = jnp.exp(run_max - next_max)
    next_sum = run_sum * rescale + jnp.einsum(
        "rb,sbh->srh", member_float, page_sum, precision=highest
    )
    added = jnp.einsum(
        "rb,sbx->srx", member_float, page_out.reshape(nsteps, nblock, nheads * head_size),
        precision=highest,
    )
    next_out = run_out * rescale[..., None] + added.reshape(nsteps, requests, nheads, head_size)
    return (next_max, next_sum, next_out)


def attend_new(carry_state, queries, new_keys, new_values, slopes, token_step):
    run_max, run_sum, run_out = carry_state
    head_size = queries.shape[2]
    for earlier in range(token_step + 1):
        scores = jnp.sum(
            queries.astype(jnp.float32) * new_keys[earlier].astype(jnp.float32), axis=2
        ) * head_size ** (-0.5)
        scores = scores - slopes[None, :] * float(token_step - earlier)
        next_max = jnp.maximum(run_max, scores)
        rescale = jnp.exp(run_max - next_max)
        expon = jnp.exp(scores - next_max)
        weights = lax.optimization_barrier(expon.astype(jnp.bfloat16)).astype(jnp.float32)
        run_sum = run_sum * rescale + expon
        run_out = run_out * rescale[:, :, None] + weights[:, :, None] * new_values[earlier].astype(
            jnp.float32
        )
        run_max = next_max
    attended = (run_out / run_sum[:, :, None]).astype(jnp.bfloat16)
    return attended.reshape(attended.shape[0], -1)


def gather_rows(part, nseq):
    copies = jnp.broadcast_to(part[None], (nseq,) + part.shape)
    return lax.all_to_all(copies, "seq", 0, 0, tiled=True)


def gather_cols(part, nseq):
    got = gather_rows(part, nseq)
    return jnp.moveaxis(got, 0, -2).reshape(part.shape[:-1] + (nseq * part.shape[-1],))


def head_sum(part, nhead):
    my_index = lax.axis_index("head")
    stride = 1
    while stride < nhead:
        other = lax.ppermute(part, "head", [(i, i ^ stride) for i in range(nhead)])
        low = (my_index & stride) == 0
        part = jnp.where(low, part + other, other + part)
        stride *= 2
    return part


def full_normalize(rows, gain_full):
    row_float = rows.astype(jnp.float32)
    totals = (jnp.sum(row_float, axis=1), jnp.sum(row_float * row_float, axis=1))
    return normalize(rows, gain_full, totals, rows.shape[1])


def butterfly_combine(state, nseq):
    my_index = lax.axis_index("seq")
    stride = 1
    while stride < nseq:
        pairs = [(i, i ^ stride) for i in range(nseq)]
        other = lax.ppermute(state, "seq", pairs)
        low = (my_index & stride) == 0
        first = tuple(jnp.where(low, a, b) for a, b in zip(state, other))
        second = tuple(jnp.where(low, b, a) for a, b in zip(state, other))
        top = jnp.maximum(first[0], second[0])
        scale_a = jnp.exp(first[0] - top)
        scale_b = jnp.exp(second[0] - top)
        total = first[1] * scale_a + second[1] * scale_b
        out = first[2] * scale_a[:, :, None] + second[2] * scale_b[:, :, None]
        state = (top, total, out)
        stride *= 2
    return state


def attend_rows(carry_state, queries, new_keys, new_values, slopes, token_step):
    run_max, run_sum, run_out = carry_state
    head_size = queries.shape[2]
    for earlier in range(len(new_keys)):
        active = earlier <= token_step
        scores = jnp.sum(
            queries.astype(jnp.float32) * new_keys[earlier].astype(jnp.float32), axis=2
        ) * head_size ** (-0.5)
        scores = scores - slopes[None, :] * (token_step - earlier).astype(jnp.float32)
        next_max = jnp.maximum(run_max, scores)
        rescale = jnp.exp(run_max - next_max)
        expon = jnp.exp(scores - next_max)
        weights = lax.optimization_barrier(expon.astype(jnp.bfloat16)).astype(jnp.float32)
        next_sum = run_sum * rescale + expon
        next_out = run_out * rescale[:, :, None] + weights[:, :, None] * new_values[earlier].astype(
            jnp.float32
        )
        run_sum = jnp.where(active, next_sum, run_sum)
        run_out = jnp.where(active, next_out, run_out)
        run_max = jnp.where(active, next_max, run_max)
    attended = (run_out / run_sum[:, :, None]).astype(jnp.bfloat16)
    return attended.reshape(attended.shape[0], -1)


def on_device(
    tokens,
    lengths,
    page_owner,
    page_number,
    key_pages,
    value_pages,
    alibi_slopes,
    norm1_gain,
    norm2_gain,
    w_qkv,
    w_out,
    w_up,
    w_down,
    nseq,
    nhead,
):
    nsteps, requests, local_width = tokens.shape
    nheads = alibi_slopes.shape[0]
    head_width = key_pages.shape[2]
    head_size = head_width // nheads
    qkv_width = w_qkv.shape[1] * w_qkv.shape[2]
    rows = nsteps * requests

    qkv_chunk = qkv_width // nseq
    up_chunk = w_up.shape[1] // nseq
    gain_pair = jnp.stack([norm1_gain, norm2_gain])
    gain_parts = []
    for _ in range(3):
        piece = lax.optimization_barrier(gain_pair.astype(jnp.bfloat16))
        gain_parts.append(piece)
        gain_pair = gain_pair - piece.astype(jnp.float32)

    token_rows = tokens.reshape(rows, local_width)
    token_float = token_rows.astype(jnp.float32)
    pad_width = max(local_width, qkv_chunk + 6, up_chunk)

    def lanes(block):
        return jnp.pad(block, [(0, 0)] * (block.ndim - 1) + [(0, pad_width - block.shape[-1])])

    gain_cols = jnp.concatenate(gain_parts, axis=0).T
    split = head_width // nseq
    qkv_block = jnp.transpose(w_qkv.reshape(local_width, 3, nseq, split), (2, 0, 1, 3)).reshape(
        nseq, local_width, qkv_chunk
    )
    qkv_block = jnp.concatenate(
        [qkv_block, jnp.broadcast_to(gain_cols[None], (nseq,) + gain_cols.shape)], axis=2
    )
    payload = jnp.concatenate(
        [
            jnp.broadcast_to(lanes(token_rows)[None], (nseq, rows, pad_width)),
            lanes(qkv_block),
            lanes(jnp.swapaxes(w_up.reshape(local_width, nseq, up_chunk), 0, 1)),
        ],
        axis=1,
    )
    got = lax.all_to_all(payload, "seq", 0, 0, tiled=True)
    gathered = jnp.moveaxis(got[:, :rows, :local_width], 0, -2).reshape(rows, nseq * local_width)
    qkv_got = got[:, rows : rows + local_width]
    qkv_cols = qkv_got[:, :, :qkv_chunk].reshape(nseq * local_width, qkv_chunk)
    pieces = qkv_got[:, :, qkv_chunk : qkv_chunk + 6].reshape(nseq * local_width, 6).T.astype(jnp.float32)
    up_cols = got[:, rows + local_width :, :up_chunk].reshape(nseq * local_width, up_chunk)
    gains = (pieces[0:2] + pieces[2:4]) + pieces[4:6]
    normed = full_normalize(gathered, gains[0])
    qkv_part = jnp.dot(normed, qkv_cols, preferred_element_type=jnp.float32).astype(jnp.bfloat16)
    all_queries = gather_cols(qkv_part[:, :split], nseq).reshape(nsteps, requests, nheads, head_size)
    kv_part = qkv_part[:, split:].astype(jnp.float32)
    own_rows = rows // nseq
    req_blocks = requests // own_rows
    kv_by_block = kv_part.reshape(nsteps, req_blocks, own_rows, 2 * split)
    kv_dest = jnp.take(kv_by_block, jnp.arange(nseq) % req_blocks, axis=1)
    kv_lanes = nsteps * own_rows * 2 * split // nheads
    kv_dest = jnp.swapaxes(kv_dest, 0, 1).reshape(nseq, nheads, kv_lanes)
    carry_state = (
        jnp.full((nsteps, requests, nheads), floor_score, jnp.float32),
        jnp.zeros((nsteps, requests, nheads), jnp.float32),
        jnp.zeros((nsteps, requests, nheads, head_size), jnp.float32),
    )

    final_state = page_block(
        carry_state, page_owner, page_number, key_pages, value_pages, all_queries, alibi_slopes, lengths
    )

    joined_state = tuple(part.reshape((rows,) + part.shape[2:]) for part in final_state)
    run_max, run_sum, run_out = joined_state
    stats = jnp.concatenate(
        [
            jnp.swapaxes(run_max.reshape(nseq, own_rows, nheads), 1, 2),
            jnp.swapaxes(run_sum.reshape(nseq, own_rows, nheads), 1, 2),
            kv_dest,
            jnp.zeros((nseq, nheads, head_size - 2 * own_rows - kv_lanes), jnp.float32),
        ],
        axis=2,
    )
    packed = jnp.concatenate(
        [run_out.reshape(nseq, own_rows, nheads, head_size), stats[:, None]], axis=1
    )
    packed = lax.all_to_all(packed, "seq", 0, 0, tiled=True)
    part_out = packed[:, :own_rows]
    part_max = jnp.swapaxes(packed[:, own_rows, :, :own_rows], 1, 2)
    part_sum = jnp.swapaxes(packed[:, own_rows, :, own_rows : 2 * own_rows], 1, 2)
    top_max = jnp.max(part_max, axis=0)
    rescale = jnp.exp(part_max - top_max[None])
    top_sum = jnp.sum(part_sum * rescale, axis=0)
    top_out = jnp.sum(part_out * rescale[:, :, :, None], axis=0)
    first_row = lax.axis_index("seq") * own_rows
    my_step = first_row // requests
    my_queries = lax.dynamic_slice_in_dim(
        all_queries.reshape(rows, nheads, head_size), first_row, own_rows, 0
    )
    kv_got = packed[:, own_rows, :, 2 * own_rows : 2 * own_rows + kv_lanes]
    kv_got = kv_got.reshape(nseq, nsteps, own_rows, 2 * split).astype(jnp.bfloat16)
    kv_got = jnp.transpose(kv_got, (1, 2, 0, 3))
    key_rows = kv_got[..., :split].reshape(nsteps, own_rows, nheads, head_size)
    value_rows = kv_got[..., split:].reshape(nsteps, own_rows, nheads, head_size)
    my_keys = [key_rows[earlier] for earlier in range(nsteps)]
    my_values = [value_rows[earlier] for earlier in range(nsteps)]
    mine = attend_rows(
        (top_max, top_sum, top_out), my_queries, my_keys, my_values, alibi_slopes, my_step
    )
    attended = gather_rows(mine, nseq).reshape(rows, -1)
    projected = head_sum(
        lax.dot_general(attended, w_out, (((1,), (1,)), ((), ())), preferred_element_type=jnp.float32),
        nhead,
    )
    hidden_in = (token_float + projected).astype(jnp.bfloat16)
    hidden_float = hidden_in.astype(jnp.float32)
    normed_two = full_normalize(gather_cols(hidden_in, nseq), gains[1])
    up_share = jnp.dot(normed_two, up_cols, preferred_element_type=jnp.float32)
    hidden_share = jax.nn.gelu(up_share, approximate=False).astype(jnp.bfloat16)
    down_part = lax.dot_general(
        gather_cols(hidden_share, nseq),
        w_down,
        (((1,), (1,)), ((), ())),
        preferred_element_type=jnp.float32,
    )
    down_proj = head_sum(down_part, nhead)
    return (hidden_float + down_proj).astype(jnp.bfloat16).reshape(nsteps, requests, local_width)


def solution(mesh):
    placed = (
        P(None, None, "seq"),
        P(),
        P("seq"),
        P("seq"),
        P("seq", None, "head"),
        P("seq", None, "head"),
        P("head"),
        P("seq"),
        P("seq"),
        P("seq", None, "head"),
        P("seq", "head"),
        P("seq", "head"),
        P("seq", "head"),
    )
    nseq = mesh.shape["seq"]
    return jax.shard_map(
        functools.partial(on_device, nseq=nseq, nhead=mesh.shape["head"]), mesh=mesh, in_specs=placed, out_specs=P(None, None, "seq"), check_vma=False
    )
```

```python
import functools

import jax
import jax.numpy as jnp
from jax import lax
from jax.sharding import PartitionSpec as P

D = 4096
BLK = 8


eps_norm = 1e-05
floor_score = -1e30
highest = lax.Precision.HIGHEST


def normalize(token_rows, gain_share, totals, width_all):
    row_sum, row_squares = totals
    mean_value = row_sum / width_all
    variance = row_squares / width_all - mean_value * mean_value
    return (
        (token_rows.astype(jnp.float32) - mean_value[:, None])
        * lax.rsqrt(variance + eps_norm)[:, None]
        * gain_share[None, :]
    ).astype(jnp.bfloat16)


def page_block(carry_state, owners, number, key_block, value_block, queries, slopes, lengths):
    run_max, run_sum, run_out = carry_state
    nblock, page_len, width_all = key_block.shape
    nheads = slopes.shape[0]
    head_size = width_all // nheads
    nsteps, requests = queries.shape[0], queries.shape[1]
    safe_owner = jnp.clip(owners, 0, requests - 1)
    page_query = jnp.take(queries, safe_owner, axis=1)
    key_heads = key_block.reshape(nblock, page_len, nheads, head_size)
    value_heads = value_block.reshape(nblock, page_len, nheads, head_size)
    scores = jnp.einsum(
        "sbhe,bthe->sbth", page_query, key_heads, preferred_element_type=jnp.float32
    ) * head_size ** (-0.5)
    positions = number[:, None] * page_len + jnp.arange(page_len, dtype=jnp.int32)[None, :]
    own_length = jnp.take(lengths, safe_owner)
    step_ids = jnp.arange(nsteps, dtype=jnp.int32)
    distance = (
        own_length[None, :, None] + step_ids[:, None, None] - positions[None]
    ).astype(jnp.float32)
    scores = scores - distance[..., None] * slopes
    valid_mask = (owners[:, None] >= 0) & (positions < own_length[:, None])
    masked = jnp.where(valid_mask[None, :, :, None], scores, floor_score)
    page_max = jnp.max(masked, axis=2)
    member = owners[None, :] == jnp.arange(requests, dtype=jnp.int32)[:, None]
    block_max = jnp.max(
        jnp.where(member[None, :, :, None], page_max[:, None, :, :], floor_score), axis=2
    )
    next_max = jnp.maximum(run_max, block_max)
    owner_max = jnp.take(next_max, safe_owner, axis=1)
    expon = jnp.where(
        valid_mask[None, :, :, None], jnp.exp(masked - owner_max[:, :, None, :]), 0.0
    )
    page_sum = jnp.sum(expon, axis=2)
    weights = expon.astype(jnp.bfloat16)
    page_out = jnp.einsum(
        "sbth,bthe->sbhe", weights, value_heads, preferred_element_type=jnp.float32
    )
    member_float = member.astype(jnp.float32)
    rescale = jnp.exp(run_max - next_max)
    next_sum = run_sum * rescale + jnp.einsum(
        "rb,sbh->srh", member_float, page_sum, precision=highest
    )
    added = jnp.einsum(
        "rb,sbx->srx", member_float, page_out.reshape(nsteps, nblock, nheads * head_size),
        precision=highest,
    )
    next_out = run_out * rescale[..., None] + added.reshape(nsteps, requests, nheads, head_size)
    return (next_max, next_sum, next_out)


def attend_new(carry_state, queries, new_keys, new_values, slopes, token_step):
    run_max, run_sum, run_out = carry_state
    head_size = queries.shape[2]
    for earlier in range(token_step + 1):
        scores = jnp.sum(
            queries.astype(jnp.float32) * new_keys[earlier].astype(jnp.float32), axis=2
        ) * head_size ** (-0.5)
        scores = scores - slopes[None, :] * float(token_step - earlier)
        next_max = jnp.maximum(run_max, scores)
        rescale = jnp.exp(run_max - next_max)
        expon = jnp.exp(scores - next_max)
        weights = lax.optimization_barrier(expon.astype(jnp.bfloat16)).astype(jnp.float32)
        run_sum = run_sum * rescale + expon
        run_out = run_out * rescale[:, :, None] + weights[:, :, None] * new_values[earlier].astype(
            jnp.float32
        )
        run_max = next_max
    attended = (run_out / run_sum[:, :, None]).astype(jnp.bfloat16)
    return attended.reshape(attended.shape[0], -1)


def gather_rows(part, nseq):
    copies = jnp.broadcast_to(part[None], (nseq,) + part.shape)
    return lax.all_to_all(copies, "seq", 0, 0, tiled=True)


def gather_cols(part, nseq):
    got = gather_rows(part, nseq)
    return jnp.moveaxis(got, 0, -2).reshape(part.shape[:-1] + (nseq * part.shape[-1],))


def head_sum(part, nhead):
    my_index = lax.axis_index("head")
    stride = 1
    while stride < nhead:
        other = lax.ppermute(part, "head", [(i, i ^ stride) for i in range(nhead)])
        low = (my_index & stride) == 0
        part = jnp.where(low, part + other, other + part)
        stride *= 2
    return part


def full_normalize(rows, gain_full):
    row_float = rows.astype(jnp.float32)
    totals = (jnp.sum(row_float, axis=1), jnp.sum(row_float * row_float, axis=1))
    return normalize(rows, gain_full, totals, rows.shape[1])


def butterfly_combine(state, nseq):
    my_index = lax.axis_index("seq")
    stride = 1
    while stride < nseq:
        pairs = [(i, i ^ stride) for i in range(nseq)]
        other = lax.ppermute(state, "seq", pairs)
        low = (my_index & stride) == 0
        first = tuple(jnp.where(low, a, b) for a, b in zip(state, other))
        second = tuple(jnp.where(low, b, a) for a, b in zip(state, other))
        top = jnp.maximum(first[0], second[0])
        scale_a = jnp.exp(first[0] - top)
        scale_b = jnp.exp(second[0] - top)
        total = first[1] * scale_a + second[1] * scale_b
        out = first[2] * scale_a[:, :, None] + second[2] * scale_b[:, :, None]
        state = (top, total, out)
        stride *= 2
    return state


def attend_rows(carry_state, queries, new_keys, new_values, slopes, token_step):
    run_max, run_sum, run_out = carry_state
    head_size = queries.shape[2]
    for earlier in range(len(new_keys)):
        active = earlier <= token_step
        scores = jnp.sum(
            queries.astype(jnp.float32) * new_keys[earlier].astype(jnp.float32), axis=2
        ) * head_size ** (-0.5)
        scores = scores - slopes[None, :] * (token_step - earlier).astype(jnp.float32)
        next_max = jnp.maximum(run_max, scores)
        rescale = jnp.exp(run_max - next_max)
        expon = jnp.exp(scores - next_max)
        weights = lax.optimization_barrier(expon.astype(jnp.bfloat16)).astype(jnp.float32)
        next_sum = run_sum * rescale + expon
        next_out = run_out * rescale[:, :, None] + weights[:, :, None] * new_values[earlier].astype(
            jnp.float32
        )
        run_sum = jnp.where(active, next_sum, run_sum)
        run_out = jnp.where(active, next_out, run_out)
        run_max = jnp.where(active, next_max, run_max)
    attended = (run_out / run_sum[:, :, None]).astype(jnp.bfloat16)
    return attended.reshape(attended.shape[0], -1)


def on_device(
    tokens,
    lengths,
    page_owner,
    page_number,
    key_pages,
    value_pages,
    alibi_slopes,
    norm1_gain,
    norm2_gain,
    w_qkv,
    w_out,
    w_up,
    w_down,
    nseq,
    nhead,
):
    nsteps, requests, local_width = tokens.shape
    nheads = alibi_slopes.shape[0]
    head_width = key_pages.shape[2]
    head_size = head_width // nheads
    qkv_width = w_qkv.shape[1] * w_qkv.shape[2]
    rows = nsteps * requests

    qkv_chunk = qkv_width // nseq
    up_chunk = w_up.shape[1] // nseq
    gain_pair = jnp.stack([norm1_gain, norm2_gain])
    gain_parts = []
    for _ in range(3):
        piece = lax.optimization_barrier(gain_pair.astype(jnp.bfloat16))
        gain_parts.append(piece)
        gain_pair = gain_pair - piece.astype(jnp.float32)

    token_rows = tokens.reshape(rows, local_width)
    token_float = token_rows.astype(jnp.float32)
    pad_width = max(local_width, qkv_chunk + 6, up_chunk)

    def lanes(block):
        return jnp.pad(block, [(0, 0)] * (block.ndim - 1) + [(0, pad_width - block.shape[-1])])

    gain_cols = jnp.concatenate(gain_parts, axis=0).T
    split = head_width // nseq
    qkv_block = jnp.transpose(w_qkv.reshape(local_width, 3, nseq, split), (2, 0, 1, 3)).reshape(
        nseq, local_width, qkv_chunk
    )
    qkv_block = jnp.concatenate(
        [qkv_block, jnp.broadcast_to(gain_cols[None], (nseq,) + gain_cols.shape)], axis=2
    )
    payload = jnp.concatenate(
        [
            jnp.broadcast_to(lanes(token_rows)[None], (nseq, rows, pad_width)),
            lanes(qkv_block),
            lanes(jnp.swapaxes(w_up.reshape(local_width, nseq, up_chunk), 0, 1)),
        ],
        axis=1,
    )
    got = lax.all_to_all(payload, "seq", 0, 0, tiled=True)
    gathered = jnp.moveaxis(got[:, :rows, :local_width], 0, -2).reshape(rows, nseq * local_width)
    qkv_got = got[:, rows : rows + local_width]
    qkv_cols = qkv_got[:, :, :qkv_chunk].reshape(nseq * local_width, qkv_chunk)
    pieces = qkv_got[:, :, qkv_chunk : qkv_chunk + 6].reshape(nseq * local_width, 6).T.astype(jnp.float32)
    up_cols = got[:, rows + local_width :, :up_chunk].reshape(nseq * local_width, up_chunk)
    gains = (pieces[0:2] + pieces[2:4]) + pieces[4:6]
    normed = full_normalize(gathered, gains[0])
    qkv_part = jnp.dot(normed, qkv_cols, preferred_element_type=jnp.float32).astype(jnp.bfloat16)
    all_queries = gather_cols(qkv_part[:, :split], nseq).reshape(nsteps, requests, nheads, head_size)
    kv_part = qkv_part[:, split:].astype(jnp.float32)
    own_rows = rows // nseq
    req_blocks = requests // own_rows
    kv_by_block = kv_part.reshape(nsteps, req_blocks, own_rows, 2 * split)
    kv_dest = jnp.take(kv_by_block, jnp.arange(nseq) % req_blocks, axis=1)
    kv_got = lax.all_to_all(jnp.swapaxes(kv_dest, 0, 1).astype(jnp.bfloat16), "seq", 0, 0, tiled=True)
    kv_got = jnp.transpose(kv_got, (1, 2, 0, 3))
    key_rows = kv_got[..., :split].reshape(nsteps, own_rows, nheads, head_size)
    value_rows = kv_got[..., split:].reshape(nsteps, own_rows, nheads, head_size)
    carry_state = (
        jnp.full((nsteps, requests, nheads), floor_score, jnp.float32),
        jnp.zeros((nsteps, requests, nheads), jnp.float32),
        jnp.zeros((nsteps, requests, nheads, head_size), jnp.float32),
    )

    final_state = page_block(
        carry_state, page_owner, page_number, key_pages, value_pages, all_queries, alibi_slopes, lengths
    )

    joined_state = tuple(part.reshape((rows,) + part.shape[2:]) for part in final_state)
    run_max, run_sum, run_out = joined_state
    stats = jnp.concatenate(
        [
            jnp.swapaxes(run_max.reshape(nseq, own_rows, nheads), 1, 2),
            jnp.swapaxes(run_sum.reshape(nseq, own_rows, nheads), 1, 2),
            jnp.zeros((nseq, nheads, head_size - 2 * own_rows), jnp.float32),
        ],
        axis=2,
    )
    packed = jnp.concatenate(
        [run_out.reshape(nseq, own_rows, nheads, head_size), stats[:, None]], axis=1
    )
    packed = lax.all_to_all(packed, "seq", 0, 0, tiled=True)
    part_out = packed[:, :own_rows]
    part_max = jnp.swapaxes(packed[:, own_rows, :, :own_rows], 1, 2)
    part_sum = jnp.swapaxes(packed[:, own_rows, :, own_rows : 2 * own_rows], 1, 2)
    top_max = jnp.max(part_max, axis=0)
    rescale = jnp.exp(part_max - top_max[None])
    top_sum = jnp.sum(part_sum * rescale, axis=0)
    top_out = jnp.sum(part_out * rescale[:, :, :, None], axis=0)
    first_row = lax.axis_index("seq") * own_rows
    my_step = first_row // requests
    my_queries = lax.dynamic_slice_in_dim(
        all_queries.reshape(rows, nheads, head_size), first_row, own_rows, 0
    )
    my_keys = [key_rows[earlier] for earlier in range(nsteps)]
    my_values = [value_rows[earlier] for earlier in range(nsteps)]
    mine = attend_rows(
        (top_max, top_sum, top_out), my_queries, my_keys, my_values, alibi_slopes, my_step
    )
    attended = gather_rows(mine, nseq).reshape(rows, -1)
    projected = head_sum(
        lax.dot_general(attended, w_out, (((1,), (1,)), ((), ())), preferred_element_type=jnp.float32),
        nhead,
    )
    hidden_in = (token_float + projected).astype(jnp.bfloat16)
    hidden_float = hidden_in.astype(jnp.float32)
    normed_two = full_normalize(gather_cols(hidden_in, nseq), gains[1])
    up_share = jnp.dot(normed_two, up_cols, preferred_element_type=jnp.float32)
    hidden_share = jax.nn.gelu(up_share, approximate=False).astype(jnp.bfloat16)
    down_part = lax.dot_general(
        gather_cols(hidden_share, nseq),
        w_down,
        (((1,), (1,)), ((), ())),
        preferred_element_type=jnp.float32,
    )
    down_proj = head_sum(down_part, nhead)
    return (hidden_float + down_proj).astype(jnp.bfloat16).reshape(nsteps, requests, local_width)


def solution(mesh):
    placed = (
        P(None, None, "seq"),
        P(),
        P("seq"),
        P("seq"),
        P("seq", None, "head"),
        P("seq", None, "head"),
        P("head"),
        P("seq"),
        P("seq"),
        P("seq", None, "head"),
        P("seq", "head"),
        P("seq", "head"),
        P("seq", "head"),
    )
    nseq = mesh.shape["seq"]
    return jax.shard_map(
        functools.partial(on_device, nseq=nseq, nhead=mesh.shape["head"]), mesh=mesh, in_specs=placed, out_specs=P(None, None, "seq"), check_vma=False
    )
```

```python
import functools

import jax
import jax.numpy as jnp
from jax import lax
from jax.sharding import PartitionSpec as P

D = 4096
BLK = 8


eps_norm = 1e-05
floor_score = -1e30
highest = lax.Precision.HIGHEST


def normalize(token_rows, gain_share, totals, width_all):
    row_sum, row_squares = totals
    mean_value = row_sum / width_all
    variance = row_squares / width_all - mean_value * mean_value
    return (
        (token_rows.astype(jnp.float32) - mean_value[:, None])
        * lax.rsqrt(variance + eps_norm)[:, None]
        * gain_share[None, :]
    ).astype(jnp.bfloat16)


def page_block(carry_state, owners, number, key_block, value_block, queries, slopes, lengths):
    run_max, run_sum, run_out = carry_state
    nblock, page_len, width_all = key_block.shape
    nheads = slopes.shape[0]
    head_size = width_all // nheads
    nsteps, requests = queries.shape[0], queries.shape[1]
    safe_owner = jnp.clip(owners, 0, requests - 1)
    page_query = jnp.take(queries, safe_owner, axis=1)
    key_heads = key_block.reshape(nblock, page_len, nheads, head_size)
    value_heads = value_block.reshape(nblock, page_len, nheads, head_size)
    scores = jnp.einsum(
        "sbhe,bthe->sbth", page_query, key_heads, preferred_element_type=jnp.float32
    ) * head_size ** (-0.5)
    positions = number[:, None] * page_len + jnp.arange(page_len, dtype=jnp.int32)[None, :]
    own_length = jnp.take(lengths, safe_owner)
    step_ids = jnp.arange(nsteps, dtype=jnp.int32)
    distance = (
        own_length[None, :, None] + step_ids[:, None, None] - positions[None]
    ).astype(jnp.float32)
    scores = scores - distance[..., None] * slopes
    valid_mask = (owners[:, None] >= 0) & (positions < own_length[:, None])
    masked = jnp.where(valid_mask[None, :, :, None], scores, floor_score)
    page_max = jnp.max(masked, axis=2)
    member = owners[None, :] == jnp.arange(requests, dtype=jnp.int32)[:, None]
    block_max = jnp.max(
        jnp.where(member[None, :, :, None], page_max[:, None, :, :], floor_score), axis=2
    )
    next_max = jnp.maximum(run_max, block_max)
    owner_max = jnp.take(next_max, safe_owner, axis=1)
    expon = jnp.where(
        valid_mask[None, :, :, None], jnp.exp(masked - owner_max[:, :, None, :]), 0.0
    )
    page_sum = jnp.sum(expon, axis=2)
    weights = expon.astype(jnp.bfloat16)
    page_out = jnp.einsum(
        "sbth,bthe->sbhe", weights, value_heads, preferred_element_type=jnp.float32
    )
    member_float = member.astype(jnp.float32)
    rescale = jnp.exp(run_max - next_max)
    next_sum = run_sum * rescale + jnp.einsum(
        "rb,sbh->srh", member_float, page_sum, precision=highest
    )
    added = jnp.einsum(
        "rb,sbx->srx", member_float, page_out.reshape(nsteps, nblock, nheads * head_size),
        precision=highest,
    )
    next_out = run_out * rescale[..., None] + added.reshape(nsteps, requests, nheads, head_size)
    return (next_max, next_sum, next_out)


def attend_new(carry_state, queries, new_keys, new_values, slopes, token_step):
    run_max, run_sum, run_out = carry_state
    head_size = queries.shape[2]
    for earlier in range(token_step + 1):
        scores = jnp.sum(
            queries.astype(jnp.float32) * new_keys[earlier].astype(jnp.float32), axis=2
        ) * head_size ** (-0.5)
        scores = scores - slopes[None, :] * float(token_step - earlier)
        next_max = jnp.maximum(run_max, scores)
        rescale = jnp.exp(run_max - next_max)
        expon = jnp.exp(scores - next_max)
        weights = lax.optimization_barrier(expon.astype(jnp.bfloat16)).astype(jnp.float32)
        run_sum = run_sum * rescale + expon
        run_out = run_out * rescale[:, :, None] + weights[:, :, None] * new_values[earlier].astype(
            jnp.float32
        )
        run_max = next_max
    attended = (run_out / run_sum[:, :, None]).astype(jnp.bfloat16)
    return attended.reshape(attended.shape[0], -1)


def gather_rows(part, nseq):
    copies = jnp.broadcast_to(part[None], (nseq,) + part.shape)
    return lax.all_to_all(copies, "seq", 0, 0, tiled=True)


def gather_cols(part, nseq):
    got = gather_rows(part, nseq)
    return jnp.moveaxis(got, 0, -2).reshape(part.shape[:-1] + (nseq * part.shape[-1],))


def head_sum(part, nhead):
    my_index = lax.axis_index("head")
    stride = 1
    while stride < nhead:
        other = lax.ppermute(part, "head", [(i, i ^ stride) for i in range(nhead)])
        low = (my_index & stride) == 0
        part = jnp.where(low, part + other, other + part)
        stride *= 2
    return part


def full_normalize(rows, gain_full):
    row_float = rows.astype(jnp.float32)
    totals = (jnp.sum(row_float, axis=1), jnp.sum(row_float * row_float, axis=1))
    return normalize(rows, gain_full, totals, rows.shape[1])


def butterfly_combine(state, nseq):
    my_index = lax.axis_index("seq")
    stride = 1
    while stride < nseq:
        pairs = [(i, i ^ stride) for i in range(nseq)]
        other = lax.ppermute(state, "seq", pairs)
        low = (my_index & stride) == 0
        first = tuple(jnp.where(low, a, b) for a, b in zip(state, other))
        second = tuple(jnp.where(low, b, a) for a, b in zip(state, other))
        top = jnp.maximum(first[0], second[0])
        scale_a = jnp.exp(first[0] - top)
        scale_b = jnp.exp(second[0] - top)
        total = first[1] * scale_a + second[1] * scale_b
        out = first[2] * scale_a[:, :, None] + second[2] * scale_b[:, :, None]
        state = (top, total, out)
        stride *= 2
    return state


def attend_rows(carry_state, queries, new_keys, new_values, slopes, token_step):
    run_max, run_sum, run_out = carry_state
    head_size = queries.shape[2]
    for earlier in range(len(new_keys)):
        active = earlier <= token_step
        scores = jnp.sum(
            queries.astype(jnp.float32) * new_keys[earlier].astype(jnp.float32), axis=2
        ) * head_size ** (-0.5)
        scores = scores - slopes[None, :] * (token_step - earlier).astype(jnp.float32)
        next_max = jnp.maximum(run_max, scores)
        rescale = jnp.exp(run_max - next_max)
        expon = jnp.exp(scores - next_max)
        weights = lax.optimization_barrier(expon.astype(jnp.bfloat16)).astype(jnp.float32)
        next_sum = run_sum * rescale + expon
        next_out = run_out * rescale[:, :, None] + weights[:, :, None] * new_values[earlier].astype(
            jnp.float32
        )
        run_sum = jnp.where(active, next_sum, run_sum)
        run_out = jnp.where(active, next_out, run_out)
        run_max = jnp.where(active, next_max, run_max)
    attended = (run_out / run_sum[:, :, None]).astype(jnp.bfloat16)
    return attended.reshape(attended.shape[0], -1)


def on_device(
    tokens,
    lengths,
    page_owner,
    page_number,
    key_pages,
    value_pages,
    alibi_slopes,
    norm1_gain,
    norm2_gain,
    w_qkv,
    w_out,
    w_up,
    w_down,
    nseq,
    nhead,
):
    nsteps, requests, local_width = tokens.shape
    nheads = alibi_slopes.shape[0]
    head_width = key_pages.shape[2]
    head_size = head_width // nheads
    qkv_width = w_qkv.shape[1] * w_qkv.shape[2]
    rows = nsteps * requests

    qkv_chunk = qkv_width // nseq
    up_chunk = w_up.shape[1] // nseq
    gain_pair = jnp.stack([norm1_gain, norm2_gain])
    gain_parts = []
    for _ in range(3):
        piece = lax.optimization_barrier(gain_pair.astype(jnp.bfloat16))
        gain_parts.append(piece)
        gain_pair = gain_pair - piece.astype(jnp.float32)

    token_rows = tokens.reshape(rows, local_width)
    token_float = token_rows.astype(jnp.float32)
    pad_width = max(local_width, qkv_chunk + 6, up_chunk)

    def lanes(block):
        return jnp.pad(block, [(0, 0)] * (block.ndim - 1) + [(0, pad_width - block.shape[-1])])

    gain_cols = jnp.concatenate(gain_parts, axis=0).T
    split = head_width // nseq
    qkv_block = jnp.transpose(w_qkv.reshape(local_width, 3, nseq, split), (2, 0, 1, 3)).reshape(
        nseq, local_width, qkv_chunk
    )
    qkv_block = jnp.concatenate(
        [qkv_block, jnp.broadcast_to(gain_cols[None], (nseq,) + gain_cols.shape)], axis=2
    )
    payload = jnp.concatenate(
        [
            jnp.broadcast_to(lanes(token_rows)[None], (nseq, rows, pad_width)),
            lanes(qkv_block),
            lanes(jnp.swapaxes(w_up.reshape(local_width, nseq, up_chunk), 0, 1)),
        ],
        axis=1,
    )
    got = lax.all_to_all(payload, "seq", 0, 0, tiled=True)
    gathered = jnp.moveaxis(got[:, :rows, :local_width], 0, -2).reshape(rows, nseq * local_width)
    qkv_got = got[:, rows : rows + local_width]
    qkv_cols = qkv_got[:, :, :qkv_chunk].reshape(nseq * local_width, qkv_chunk)
    pieces = qkv_got[:, :, qkv_chunk : qkv_chunk + 6].reshape(nseq * local_width, 6).T.astype(jnp.float32)
    up_cols = got[:, rows + local_width :, :up_chunk].reshape(nseq * local_width, up_chunk)
    gains = (pieces[0:2] + pieces[2:4]) + pieces[4:6]
    normed = full_normalize(gathered, gains[0])
    qkv_part = jnp.dot(normed, qkv_cols, preferred_element_type=jnp.float32).astype(jnp.bfloat16)
    kv_part = qkv_part[:, split:].astype(jnp.float32)
    own_rows = rows // nseq
    req_blocks = requests // own_rows
    kv_by_block = kv_part.reshape(nsteps, req_blocks, own_rows, 2 * split)
    kv_dest = jnp.take(kv_by_block, jnp.arange(nseq) % req_blocks, axis=1)
    q_part = qkv_part[:, :split]
    kv_flat = jnp.swapaxes(kv_dest, 0, 1).astype(jnp.bfloat16).reshape(nseq, -1, split)
    q_payload = jnp.concatenate(
        [jnp.broadcast_to(q_part[None], (nseq,) + q_part.shape), kv_flat], axis=1
    )
    q_got = lax.all_to_all(q_payload, "seq", 0, 0, tiled=True)
    all_queries = jnp.moveaxis(q_got[:, :rows], 0, -2).reshape(nsteps, requests, nheads, head_size)
    kv_got = q_got[:, rows:].reshape(nseq, nsteps, own_rows, 2 * split)
    kv_got = jnp.transpose(kv_got, (1, 2, 0, 3))
    key_rows = kv_got[..., :split].reshape(nsteps, own_rows, nheads, head_size)
    value_rows = kv_got[..., split:].reshape(nsteps, own_rows, nheads, head_size)
    carry_state = (
        jnp.full((nsteps, requests, nheads), floor_score, jnp.float32),
        jnp.zeros((nsteps, requests, nheads), jnp.float32),
        jnp.zeros((nsteps, requests, nheads, head_size), jnp.float32),
    )

    final_state = page_block(
        carry_state, page_owner, page_number, key_pages, value_pages, all_queries, alibi_slopes, lengths
    )

    joined_state = tuple(part.reshape((rows,) + part.shape[2:]) for part in final_state)
    run_max, run_sum, run_out = joined_state
    stats = jnp.concatenate(
        [
            jnp.swapaxes(run_max.reshape(nseq, own_rows, nheads), 1, 2),
            jnp.swapaxes(run_sum.reshape(nseq, own_rows, nheads), 1, 2),
            jnp.zeros((nseq, nheads, head_size - 2 * own_rows), jnp.float32),
        ],
        axis=2,
    )
    packed = jnp.concatenate(
        [run_out.reshape(nseq, own_rows, nheads, head_size), stats[:, None]], axis=1
    )
    packed = lax.all_to_all(packed, "seq", 0, 0, tiled=True)
    part_out = packed[:, :own_rows]
    part_max = jnp.swapaxes(packed[:, own_rows, :, :own_rows], 1, 2)
    part_sum = jnp.swapaxes(packed[:, own_rows, :, own_rows : 2 * own_rows], 1, 2)
    top_max = jnp.max(part_max, axis=0)
    rescale = jnp.exp(part_max - top_max[None])
    top_sum = jnp.sum(part_sum * rescale, axis=0)
    top_out = jnp.sum(part_out * rescale[:, :, :, None], axis=0)
    first_row = lax.axis_index("seq") * own_rows
    my_step = first_row // requests
    my_queries = lax.dynamic_slice_in_dim(
        all_queries.reshape(rows, nheads, head_size), first_row, own_rows, 0
    )
    my_keys = [key_rows[earlier] for earlier in range(nsteps)]
    my_values = [value_rows[earlier] for earlier in range(nsteps)]
    mine = attend_rows(
        (top_max, top_sum, top_out), my_queries, my_keys, my_values, alibi_slopes, my_step
    )
    attended = gather_rows(mine, nseq).reshape(rows, -1)
    projected = head_sum(
        lax.dot_general(attended, w_out, (((1,), (1,)), ((), ())), preferred_element_type=jnp.float32),
        nhead,
    )
    hidden_in = (token_float + projected).astype(jnp.bfloat16)
    hidden_float = hidden_in.astype(jnp.float32)
    normed_two = full_normalize(gather_cols(hidden_in, nseq), gains[1])
    up_share = jnp.dot(normed_two, up_cols, preferred_element_type=jnp.float32)
    hidden_share = jax.nn.gelu(up_share, approximate=False).astype(jnp.bfloat16)
    down_part = lax.dot_general(
        gather_cols(hidden_share, nseq),
        w_down,
        (((1,), (1,)), ((), ())),
        preferred_element_type=jnp.float32,
    )
    down_proj = head_sum(down_part, nhead)
    return (hidden_float + down_proj).astype(jnp.bfloat16).reshape(nsteps, requests, local_width)


def solution(mesh):
    placed = (
        P(None, None, "seq"),
        P(),
        P("seq"),
        P("seq"),
        P("seq", None, "head"),
        P("seq", None, "head"),
        P("head"),
        P("seq"),
        P("seq"),
        P("seq", None, "head"),
        P("seq", "head"),
        P("seq", "head"),
        P("seq", "head"),
    )
    nseq = mesh.shape["seq"]
    return jax.shard_map(
        functools.partial(on_device, nseq=nseq, nhead=mesh.shape["head"]), mesh=mesh, in_specs=placed, out_specs=P(None, None, "seq"), check_vma=False
    )
```
